512 devices in a mesh: cols: 128 (over x, z, core), mem: 4 (over y).
Axes of the slice: x: 4, y: 4, z: 16, core: 2. Of those that a mesh axis runs over, the one named last changes fastest.
Arguments:
- column_profiles: bfloat16 [2048, 100, 512], P('cols', None, 'mem'), may hold values from -6 to 6
- w_in: bfloat16 [100, 256], replicated, may hold values from -0.625 to 0.625
- w_depth: float32 [3, 256], replicated, may hold values from -3 to 3
- w_out: bfloat16 [256, 100], replicated, may hold values from -0.375 to 0.375
- obs_op: float32 [100, 16], replicated, may hold values from -0.625 to 0.625
- foot: int32 [16384, 4], P('cols'), may hold values from -1 to 15, as said below
- owner: int32 [16384, 1], P('cols'), may hold values from 0 to 127; in each aligned block of 128 rows (0 to 127, 128 to 255, ...) at most 2 rows name the same one
- obs: float32 [16384, 16], P('cols'), may hold values from -6 to 6
- rinv: float32 [16384, 16], P('cols'), may hold values from 0.5 to 4
- inflation: float32 [128], P('cols'), may hold values from 0.5 to 2
Outputs:
- analysis: bfloat16 [2048, 100, 512], P('cols', None, 'mem')
The draws below stay inside these ranges and needn't reach their ends.
Inputs may be any that keep to these rules, and one draw needn't show every extreme that they name: `foot`: the first slot of every batch is a column of its source; other slots are a column or -1. Among the 128 batches of one index of cols, no owner appears more than 2 times.
All inputs are finite; a program needn't handle non-finite values.
Results may differ from the reference program's by a relative error of at most 0.01.
Values may be sent and summed in bfloat16 or wider, within the bound.
No kernel may reach another device: no remote copies, remote signals or barrier semaphores. Data moves between devices by JAX's collectives and lax.ppermute only.
A program may use at most 64 MiB of HBM per device.

```python
import math
import jax
import jax.numpy as jnp
import numpy as np
from jax import lax

C = 100
HID = 256
ENSEMBLE_SIZE = 512
OBS = 16
FOOT = 4
COL_DEV = 16
SRC_B = 128
CAP = 2
NCOL = 2048
NB = 16384
N_COLS = 128


def draw_foot(key, part):
    first_key, second_key = jax.random.split(jax.random.fold_in(key, 17))
    columns = jax.random.randint(first_key, (NB, FOOT), 0, COL_DEV)
    keep = jax.random.randint(second_key, (NB, FOOT), 0, 2)
    keep = keep.at[:, 0].set(1)
    return jnp.where(keep == 1, columns, -1).astype(jnp.int32)


def steps_of(rng, shape, cuts, low, high):
    gain, own = 1.0, jax.random.fold_in(rng, 6)
    for dim, blocks in cuts:
        draws = jnp.exp(jax.random.uniform(jax.random.fold_in(own, dim), (blocks,), jnp.float32, low / len(cuts), high / len(cuts)))
        gain = gain * jnp.repeat(draws, shape[dim] // blocks).reshape([-1 if axis == dim else 1 for axis in range(len(shape))])
    return gain


def assign_block(own_key, own, number, rows, number_of, top, bound, slope):
    ranking = jax.random.permutation(own_key, number_of)
    packed, usual = shares(number_of, rows * top, bound, slope, True), shares(number_of, rows * top, bound, slope, False)
    places = jnp.arange(number_of)

    def named(tallies, rotation):
        used = int((tallies > 0).sum())
        fixed = max(1, used // 4)
        passed = fixed + (places - fixed + rotation * (used - fixed)) % max(1, number_of - fixed)
        return jnp.zeros((number_of,), jnp.int32).at[ranking[jnp.where(places < fixed, places, passed)]].set(jnp.asarray(tallies, jnp.int32))

    tallies = jnp.where(number % 4 == 0, named(packed, number // 4), named(usual, number - number // 4 - 1))
    mixed = jax.random.permutation(jax.random.fold_in(own, 3), number_of)
    donor, receiver = mixed[0:number_of // 2 * 2:2], mixed[1:number_of // 2 * 2:2]
    room = jnp.minimum(tallies[donor] - 1, bound - tallies[receiver]) // 2
    room = jnp.where((donor == ranking[0]) | (receiver == ranking[0]) | (tallies[receiver] == 0), 0, jnp.maximum(room, 0))
    passed = jax.random.randint(jax.random.fold_in(own, 4), (number_of // 2,), 0, 1 << 20) % (room + 1)
    tallies = tallies.at[donor].add(-passed).at[receiver].add(passed)
    labels = jnp.searchsorted(jnp.cumsum(tallies), jnp.arange(rows * top), side="right").astype(jnp.int32)
    listing = labels.reshape(top, rows).T
    listing = listing[jax.random.permutation(jax.random.fold_in(own, 1), rows)]
    rotation = jax.random.randint(jax.random.fold_in(own, 2), (rows, 1), 0, top)
    return jnp.take_along_axis(listing, (jnp.arange(top)[None, :] + rotation) % top, axis=1)


def shares(number_of, total, bound, lean, full):
    loads = [(1 << 20) // math.isqrt(rank ** lean) + 1 for rank in range(1, number_of + 1)]
    largest = bound if full else min(bound, max(-(-total // number_of), total * loads[0] // sum(loads)))
    least = 1 if total - largest >= number_of - 1 else 0
    given, spare = [largest] + [least] * (number_of - 1), total - largest - least * (number_of - 1)
    while spare > 0:
        candidates = [i for i in range(1, number_of) if given[i] < largest] or [i for i in range(1, number_of) if given[i] < bound]
        pool, remaining = sum([loads[i] for i in candidates]), spare
        for i in candidates:
            addition = min(bound - given[i], max(1, remaining * loads[i] // pool), spare)
            given[i] = given[i] + addition
            spare = spare - addition
    return np.array(given)


def scatter_about(own_key, shape, scale, limit, cuts=(), kind=jnp.bfloat16):
    values = jax.random.normal(own_key, shape, jnp.float32) * scale
    if len(cuts) > 0:
        values = steps_of(own_key, shape, cuts, -0.22, 0.18) * values
    return jnp.clip(values, min=-limit, max=limit).astype(kind)


def setup_inputs(seed: int = 0) -> dict:
    key_of = jax.random.split(jax.random.key(seed), 11)
    column_profiles = scatter_about(key_of[0], (NCOL, C, ENSEMBLE_SIZE), 1.0, 6.0, ((0, 128), (2, 4)))
    w_in = scatter_about(key_of[1], (C, HID), C ** -0.5, 0.625)
    w_depth = scatter_about(key_of[2], (3, HID), 0.6, 3.0, (), jnp.float32)
    w_out = scatter_about(key_of[3], (HID, C), HID ** -0.5, 0.375)
    obs_op = scatter_about(key_of[4], (C, OBS), C ** -0.5, 0.625, (), jnp.float32)
    foot = draw_foot(jax.random.fold_in(key_of[10], 71), 0)
    owner_keys = jax.random.split(jax.random.fold_in(key_of[6], 1), NB // SRC_B)
    owner_turns = jax.random.permutation(jax.random.fold_in(key_of[6], 3), NB // SRC_B)
    owner = jax.vmap(lambda own, number: assign_block(jax.random.fold_in(key_of[6], 2), own, number, SRC_B, N_COLS, 1, CAP, 2))(owner_keys, owner_turns).reshape((NB, 1))
    obs = scatter_about(key_of[7], (NB, OBS), 1.0, 6.0, ((0, 128),), jnp.float32)
    rinv = jnp.clip(jnp.exp(math.log(4.0) - 2.0794415 * jax.random.uniform(key_of[8], (NB, OBS), jnp.float32) ** steps_of(key_of[8], (NB, OBS), ((0, 128),), -0.2, 0.2)), 0.5, 4.0)
    inflation = jnp.clip(jnp.exp(math.log(2.0) - 1.3862944 * jax.random.uniform(key_of[9], (N_COLS,), jnp.float32) ** steps_of(key_of[9], (N_COLS,), ((0, 128),), -0.2, 0.2)), 0.5, 2.0)
    return dict(column_profiles=column_profiles, w_in=w_in, w_depth=w_depth, w_out=w_out, obs_op=obs_op, foot=foot, owner=owner, obs=obs, rinv=rinv, inflation=inflation)


def reference(column_profiles, w_in, w_depth, w_out, obs_op, foot, owner, obs, rinv, inflation):
    top = lax.Precision.HIGHEST
    zeros = jnp.zeros((1, C, ENSEMBLE_SIZE), jnp.bfloat16)
    padded = jnp.concatenate([zeros, column_profiles, zeros], axis=0)

    def predicted_portion(input_profile):
        window = lax.dynamic_slice_in_dim(padded, input_profile * COL_DEV, COL_DEV + 2, 0)
        hidden = jax.nn.gelu(jnp.einsum('kcm,ch->khm', window.astype(jnp.float32), w_in.astype(jnp.float32), precision=top)).astype(jnp.bfloat16)
        mixed = (w_depth[0][None, :, None] * hidden[:-2] + w_depth[1][None, :, None] * hidden[1:-1] + w_depth[2][None, :, None] * hidden[2:]).astype(jnp.bfloat16)
        update = jnp.einsum('khm,hc->kcm', mixed.astype(jnp.float32), w_out.astype(jnp.float32), precision=top)
        return window[1:-1].astype(jnp.float32) + update
    predicted_column = lax.map(predicted_portion, jnp.arange(N_COLS, dtype=jnp.int32))
    profile_average = lax.optimization_barrier(jnp.sum(predicted_column, axis=3)) / ENSEMBLE_SIZE
    departure_from_average = predicted_column - profile_average[..., None]
    pobs = jnp.einsum('skcm,co->skom', departure_from_average, obs_op, precision=top)
    mobs = jnp.einsum('skc,co->sko', profile_average, obs_op, precision=top)
    foot3 = foot.reshape(N_COLS, SRC_B, FOOT)
    hits = (foot3[..., None] == jnp.arange(COL_DEV, dtype=jnp.int32)).astype(jnp.float32)
    counts = lax.optimization_barrier(jnp.sum((foot3 >= 0).astype(jnp.float32), axis=2))
    onehot = lax.optimization_barrier(jnp.sum(hits, axis=2)) / counts[..., None]
    fpert = jnp.einsum('sbk,skom->sbom', onehot, pobs, precision=top)
    fmean = jnp.einsum('sbk,sko->sbo', onehot, mobs, precision=top)
    scale = 1.0 / math.sqrt(ENSEMBLE_SIZE - 1)
    rinv3 = rinv.reshape(N_COLS, SRC_B, OBS)
    spread = (rinv3[..., None] * fpert * scale).astype(jnp.bfloat16).reshape(NB, OBS, ENSEMBLE_SIZE)
    innov = (rinv3 * (obs.reshape(N_COLS, SRC_B, OBS) - fmean)).astype(jnp.bfloat16).reshape(NB, OBS)
    factor = inflation[owner[:, 0]] ** 2
    spread32 = spread.astype(jnp.float32)
    weighted = spread32 * factor[:, None, None]
    gram = jnp.eye(ENSEMBLE_SIZE, dtype=jnp.float32) + jnp.einsum('bom,boj->mj', weighted, spread32, precision=top)
    vec = jnp.einsum('bom,bo->m', weighted, innov.astype(jnp.float32), precision=top)
    chol = jnp.linalg.cholesky(gram)
    weights = jax.scipy.linalg.cho_solve((chol, True), vec)
    tinv = jax.scipy.linalg.solve_triangular(chol.T, jnp.eye(ENSEMBLE_SIZE, dtype=jnp.float32), lower=False)
    mix_w = (weights[:, None] * scale + tinv).astype(jnp.bfloat16)
    pertb = departure_from_average.astype(jnp.bfloat16)

    def analyse(pair):
        mean_block, pert_block = pair
        moved = jnp.einsum('kcm,mj->kcj', pert_block.astype(jnp.float32), mix_w.astype(jnp.float32), precision=top)
        return (mean_block[:, :, None] + moved).astype(jnp.bfloat16)
    analysis = lax.map(analyse, (profile_average, pertb))
    return analysis.reshape(N_COLS * COL_DEV, C, ENSEMBLE_SIZE)
```

```python
import math

import jax
import jax.numpy as jnp
from jax import lax
from jax.experimental import pallas as pl
from jax.experimental.pallas import tpu as pltpu
from jax.sharding import PartitionSpec as P


def extended(block, sides, width):
    for axis, dim in sides:
        count = lax.axis_size(axis)
        forward = [(i, i + 1) for i in range(count - 1)]
        backward = [(target, source) for source, target in forward]
        low = lax.ppermute(
            lax.slice_in_dim(block, block.shape[dim] - width, None, axis=dim), axis, forward
        )
        high = lax.ppermute(lax.slice_in_dim(block, 0, width, axis=dim), axis, backward)
        block = jnp.concatenate([low, block, high], axis=dim)
    return block


def sent_to_all(shard, axis):
    peers = lax.axis_size(axis)
    return lax.all_to_all(
        jnp.broadcast_to(shard[None], (peers, *shard.shape)), axis, 0, 0, tiled=True
    )


def taken_together(shard, axis):
    everything = sent_to_all(shard, axis)
    return jnp.sum(everything, axis=0)


def in_one_piece(arrays, axis, split_dim, concat_dim, along):
    columns = [a.reshape(*a.shape[:along], -1) for a in arrays]
    both = jnp.concatenate(columns, axis=along)
    out, at, done = (
        lax.all_to_all(both, axis, split_axis=split_dim, concat_axis=concat_dim, tiled=True),
        0,
        [],
    )
    for a, column in zip(arrays, columns):
        section = out[..., at : at + column.shape[along]]
        done.append(section.reshape(*section.shape[:along], *a.shape[along:]))
        at += column.shape[along]
    return tuple(done)


def in_one_piece_2(arrays, axis, split_dim, concat_dim, along):
    ends, at = ([], 0)
    for a in arrays[:-1]:
        at += a.shape[along]
        ends.append(at)
    both = jnp.concatenate(arrays, axis=along)
    return tuple(
        jnp.split(
            lax.all_to_all(both, axis, split_axis=split_dim, concat_axis=concat_dim, tiled=True),
            ends,
            axis=along,
        )
    )


def together(arrays, axis):
    ravelled, at, done = (jnp.concatenate([a.reshape(-1) for a in arrays]), 0, [])
    subtotal = lax.psum(ravelled, axis)
    for a in arrays:
        done.append(subtotal[at : at + a.size].reshape(a.shape))
        at += a.size
    return tuple(done)


def joined_along(parts, dim):
    parts = jnp.moveaxis(parts, 0, dim)
    lengths = parts.shape
    return parts.reshape(*lengths[:dim], lengths[dim] * lengths[dim + 1], *lengths[dim + 2 :])


def collect(shard, axis, dim):
    return joined_along(sent_to_all(shard, axis), dim)


def _eliminate(a_ref, low_ref, inv_ref, m_ref):
    n = a_ref.shape[0]
    sub = lax.broadcasted_iota(jnp.int32, (n, 1), 0)
    lane = lax.broadcasted_iota(jnp.int32, (1, n), 1)
    rows = lax.broadcasted_iota(jnp.int32, (n, n), 0)
    cols = lax.broadcasted_iota(jnp.int32, (n, n), 1)
    m_ref[:, :n] = a_ref[...]
    m_ref[:, n:] = (rows == cols).astype(jnp.float32)

    def step(j, carry):
        row = m_ref[pl.ds(j, 1), :]
        whole = m_ref[...]
        column = jnp.sum(jnp.where(lane == j, whole[:, :n], 0.0), axis=1, keepdims=True)
        pivot = jnp.sum(jnp.where(lane == j, row[:, :n], 0.0), axis=1, keepdims=True)
        factor = jnp.where(sub > j, column / pivot, 0.0)
        m_ref[...] = whole - factor * row
        return carry

    lax.fori_loop(0, n, step, 0)
    whole = m_ref[...]
    diag = jnp.sum(jnp.where(rows == cols, whole[:, :n], 0.0), axis=1, keepdims=True)
    scale = 1.0 / jnp.sqrt(diag)
    low_ref[...] = jnp.where(rows <= cols, whole[:, :n] * scale, 0.0)
    inv_ref[...] = whole[:, n:] * scale


def factor_block(block):
    width = block.shape[0]
    symmetric = jnp.tril(block) + jnp.tril(block, -1).T
    square = jax.ShapeDtypeStruct((width, width), jnp.float32)
    upper, inverse = pl.pallas_call(
        _eliminate,
        out_shape=(square, square),
        in_specs=[pl.BlockSpec(memory_space=pltpu.VMEM)],
        out_specs=(pl.BlockSpec(memory_space=pltpu.VMEM), pl.BlockSpec(memory_space=pltpu.VMEM)),
        scratch_shapes=[pltpu.VMEM((width, 2 * width), jnp.float32)],
    )(symmetric)
    return upper.T, inverse


def factor_inverse(gram):
    top = lax.Precision.HIGHEST
    order = gram.shape[0]
    step_size = min(128, order)
    identity = jnp.eye(order, dtype=jnp.float32)
    chol = jnp.zeros((order, order), jnp.float32)
    chol_inverse = jnp.zeros((order, order), jnp.float32)
    for block_index in range(order // step_size):
        begin = block_index * step_size
        finish = begin + step_size
        panel = gram[begin:, begin:finish]
        if block_index > 0:
            panel = panel - jnp.dot(
                chol[begin:, :begin], chol[begin:finish, :begin].T, precision=top
            )
        diag_low, diag_inverse = factor_block(panel[:step_size])
        below = jnp.dot(panel[step_size:], diag_inverse.T, precision=top)
        chol = chol.at[begin:, begin:finish].set(jnp.concatenate([diag_low, below], axis=0))
        right_side = identity[begin:finish]
        if block_index > 0:
            right_side = right_side - jnp.dot(
                chol[begin:finish, :begin], chol_inverse[:begin], precision=top
            )
        chol_inverse = chol_inverse.at[begin:finish].set(
            jnp.dot(diag_inverse, right_side, precision=top)
        )
    return chol_inverse


def body(column_profiles, w_in, w_depth, w_out, obs_op, foot, owner, obs, rinv, inflation):
    top = lax.Precision.HIGHEST
    n_cols = lax.axis_size("cols")
    n_mem = lax.axis_size("mem")
    mem_dev = column_profiles.shape[2]
    members = mem_dev * n_mem
    src_b = foot.shape[0]
    col_dev = column_profiles.shape[0]
    widened = extended(column_profiles, (("cols", 0),), 1)
    hidden = jax.nn.gelu(
        jnp.einsum("kcm,ch->khm", widened, w_in, preferred_element_type=jnp.float32)
    ).astype(jnp.bfloat16)
    mixed = (
        w_depth[0][None, :, None] * hidden[:-2]
        + w_depth[1][None, :, None] * hidden[1:-1]
        + w_depth[2][None, :, None] * hidden[2:]
    ).astype(jnp.bfloat16)
    predicted_column = column_profiles.astype(jnp.float32) + jnp.einsum(
        "khm,hc->kcm", mixed, w_out, preferred_element_type=jnp.float32
    )
    grand_accumulation = taken_together(jnp.sum(predicted_column, axis=2), "mem")
    profile_average = grand_accumulation / members
    departure_from_average = predicted_column - profile_average[:, :, None]
    pobs = jnp.einsum("kcm,co->kom", departure_from_average, obs_op, precision=top)
    mobs = jnp.dot(profile_average, obs_op, precision=top)
    hits = (foot[:, :, None] == jnp.arange(col_dev, dtype=jnp.int32)[None, None, :]).astype(
        jnp.float32
    )
    counts = jnp.sum((foot >= 0).astype(jnp.float32), axis=1)
    onehot = jnp.sum(hits, axis=1) / counts[:, None]
    fpert = jnp.einsum("bk,kom->bom", onehot, pobs, precision=top)
    fmean = jnp.dot(onehot, mobs, precision=top)
    scale = 1.0 / math.sqrt(members - 1)
    spread = (rinv[:, :, None] * fpert * scale).astype(jnp.bfloat16)
    innov = (rinv * (obs - fmean)).astype(jnp.bfloat16)
    target = owner[:, 0]
    capacity = max(2, 2 * src_b // n_cols)
    owner_hits = (target[:, None] == jnp.arange(n_cols, dtype=jnp.int32)[None, :]).astype(jnp.int32)
    ranking = jnp.sum((jnp.cumsum(owner_hits, axis=0) - 1) * owner_hits, axis=1)
    slot = target * capacity + ranking
    placing = (slot[:, None] == jnp.arange(n_cols * capacity, dtype=jnp.int32)[None, :]).astype(
        jnp.bfloat16
    )
    send_spread = jnp.einsum(
        "bq,bom->qom", placing, spread, preferred_element_type=jnp.float32
    ).astype(jnp.bfloat16)
    send_innov = jnp.einsum("bq,bo->qo", placing, innov, preferred_element_type=jnp.float32).astype(
        jnp.bfloat16
    )
    held_spread, held_innov = in_one_piece((send_spread, send_innov), "cols", 0, 0, 2)
    held_factor = jnp.full((held_spread.shape[0],), inflation[0] * inflation[0], jnp.float32)
    quarter = held_spread.shape[0] // n_mem
    factor_grid = jnp.broadcast_to(held_factor[:, None, None], held_spread.shape)
    portion, factor_part = tuple(
        (
            part.astype(jnp.float32)
            for part in in_one_piece_2(
                (
                    held_spread.astype(jnp.float32).astype(jnp.bfloat16),
                    factor_grid.astype(jnp.bfloat16),
                ),
                "mem",
                0,
                2,
                1,
            )
        )
    )
    innov_part = lax.dynamic_slice_in_dim(held_innov, lax.axis_index("mem") * quarter, quarter, 0)
    weighted = portion * factor_part
    whole = jnp.einsum("qom,qoj->mj", weighted, portion, precision=top)
    vector = jnp.einsum("qom,qo->m", weighted, innov_part.astype(jnp.float32), precision=top)
    gram_part, vec_all = together((whole, vector), ("cols", "mem"))
    gram = jnp.eye(members, dtype=jnp.float32) + gram_part
    chol_inverse = factor_inverse(gram)
    weights = jnp.dot(chol_inverse.T, jnp.dot(chol_inverse, vec_all, precision=top), precision=top)
    first = lax.axis_index("mem") * mem_dev
    tinv_mine = lax.dynamic_slice_in_dim(chol_inverse, first, mem_dev, 0).T
    mix_w = (weights[:, None] * scale + tinv_mine).astype(jnp.bfloat16)
    pertb = departure_from_average.astype(jnp.bfloat16)
    moved = jnp.einsum(
        "kcm,mj->kcj", collect(pertb, "mem", 2), mix_w, preferred_element_type=jnp.float32
    )
    return (profile_average[:, :, None] + moved).astype(jnp.bfloat16)


def solution(mesh):
    placed = (
        P("cols", None, "mem"),
        P(),
        P(),
        P(),
        P(),
        P("cols", None),
        P("cols", None),
        P("cols", None),
        P("cols", None),
        P("cols"),
    )
    return jax.shard_map(
        body, mesh=mesh, in_specs=placed, out_specs=P("cols", None, "mem"), check_vma=False
    )
```

```python
import math

import jax
import jax.numpy as jnp
from jax import lax
from jax.experimental import pallas as pl
from jax.experimental.pallas import tpu as pltpu
from jax.sharding import PartitionSpec as P


def extended(block, sides, width):
    for axis, dim in sides:
        count = lax.axis_size(axis)
        forward = [(i, i + 1) for i in range(count - 1)]
        backward = [(target, source) for source, target in forward]
        low = lax.ppermute(
            lax.slice_in_dim(block, block.shape[dim] - width, None, axis=dim), axis, forward
        )
        high = lax.ppermute(lax.slice_in_dim(block, 0, width, axis=dim), axis, backward)
        block = jnp.concatenate([low, block, high], axis=dim)
    return block


def sent_to_all(shard, axis):
    peers = lax.axis_size(axis)
    return lax.all_to_all(
        jnp.broadcast_to(shard[None], (peers, *shard.shape)), axis, 0, 0, tiled=True
    )


def taken_together(shard, axis):
    everything = sent_to_all(shard, axis)
    return jnp.sum(everything, axis=0)


def in_one_piece(arrays, axis, split_dim, concat_dim, along):
    columns = [a.reshape(*a.shape[:along], -1) for a in arrays]
    both = jnp.concatenate(columns, axis=along)
    out, at, done = (
        lax.all_to_all(both, axis, split_axis=split_dim, concat_axis=concat_dim, tiled=True),
        0,
        [],
    )
    for a, column in zip(arrays, columns):
        section = out[..., at : at + column.shape[along]]
        done.append(section.reshape(*section.shape[:along], *a.shape[along:]))
        at += column.shape[along]
    return tuple(done)


def in_one_piece_2(arrays, axis, split_dim, concat_dim, along):
    ends, at = ([], 0)
    for a in arrays[:-1]:
        at += a.shape[along]
        ends.append(at)
    both = jnp.concatenate(arrays, axis=along)
    return tuple(
        jnp.split(
            lax.all_to_all(both, axis, split_axis=split_dim, concat_axis=concat_dim, tiled=True),
            ends,
            axis=along,
        )
    )


def together(arrays, axis):
    ravelled, at, done = (jnp.concatenate([a.reshape(-1) for a in arrays]), 0, [])
    subtotal = lax.psum(ravelled, axis)
    for a in arrays:
        done.append(subtotal[at : at + a.size].reshape(a.shape))
        at += a.size
    return tuple(done)


def joined_along(parts, dim):
    parts = jnp.moveaxis(parts, 0, dim)
    lengths = parts.shape
    return parts.reshape(*lengths[:dim], lengths[dim] * lengths[dim + 1], *lengths[dim + 2 :])


def collect(shard, axis, dim):
    return joined_along(sent_to_all(shard, axis), dim)


def _eliminate(a_ref, low_ref, inv_ref, m_ref):
    n = a_ref.shape[0]
    sub = lax.broadcasted_iota(jnp.int32, (n, 1), 0)
    lane = lax.broadcasted_iota(jnp.int32, (1, n), 1)
    rows = lax.broadcasted_iota(jnp.int32, (n, n), 0)
    cols = lax.broadcasted_iota(jnp.int32, (n, n), 1)
    m_ref[:, :n] = a_ref[...]
    m_ref[:, n:] = (rows == cols).astype(jnp.float32)

    def step(j, carry):
        row = m_ref[pl.ds(j, 1), :]
        whole = m_ref[...]
        column = jnp.sum(jnp.where(lane == j, whole[:, :n], 0.0), axis=1, keepdims=True)
        pivot = jnp.sum(jnp.where(lane == j, row[:, :n], 0.0), axis=1, keepdims=True)
        factor = jnp.where(sub > j, column / pivot, 0.0)
        m_ref[...] = whole - factor * row
        return carry

    lax.fori_loop(0, n, step, 0)
    whole = m_ref[...]
    diag = jnp.sum(jnp.where(rows == cols, whole[:, :n], 0.0), axis=1, keepdims=True)
    scale = 1.0 / jnp.sqrt(diag)
    low_ref[...] = jnp.where(rows <= cols, whole[:, :n] * scale, 0.0)
    inv_ref[...] = whole[:, n:] * scale


def factor_block(block):
    width = block.shape[0]
    symmetric = jnp.tril(block) + jnp.tril(block, -1).T
    square = jax.ShapeDtypeStruct((width, width), jnp.float32)
    upper, inverse = pl.pallas_call(
        _eliminate,
        out_shape=(square, square),
        in_specs=[pl.BlockSpec(memory_space=pltpu.VMEM)],
        out_specs=(pl.BlockSpec(memory_space=pltpu.VMEM), pl.BlockSpec(memory_space=pltpu.VMEM)),
        scratch_shapes=[pltpu.VMEM((width, 2 * width), jnp.float32)],
    )(symmetric)
    return upper.T, inverse


def factor_inverse(gram):
    top = lax.Precision.HIGHEST
    order = gram.shape[0]
    step_size = min(128, order)
    identity = jnp.eye(order, dtype=jnp.float32)
    chol = jnp.zeros((order, order), jnp.float32)
    chol_inverse = jnp.zeros((order, order), jnp.float32)
    for block_index in range(order // step_size):
        begin = block_index * step_size
        finish = begin + step_size
        panel = gram[begin:, begin:finish]
        if block_index > 0:
            panel = panel - jnp.dot(
                chol[begin:, :begin], chol[begin:finish, :begin].T, precision=top
            )
        diag_low, diag_inverse = factor_block(panel[:step_size])
        below = jnp.dot(panel[step_size:], diag_inverse.T, precision=top)
        chol = chol.at[begin:, begin:finish].set(jnp.concatenate([diag_low, below], axis=0))
        right_side = identity[begin:finish]
        if block_index > 0:
            right_side = right_side - jnp.dot(
                chol[begin:finish, :begin], chol_inverse[:begin], precision=top
            )
        chol_inverse = chol_inverse.at[begin:finish].set(
            jnp.dot(diag_inverse, right_side, precision=top)
        )
    return chol_inverse


def body(column_profiles, w_in, w_depth, w_out, obs_op, foot, owner, obs, rinv, inflation):
    top = lax.Precision.HIGHEST
    n_cols = lax.axis_size("cols")
    n_mem = lax.axis_size("mem")
    mem_dev = column_profiles.shape[2]
    members = mem_dev * n_mem
    src_b = foot.shape[0]
    col_dev = column_profiles.shape[0]
    widened = extended(column_profiles, (("cols", 0),), 1)
    hidden = jax.nn.gelu(
        jnp.einsum("kcm,ch->khm", widened, w_in, preferred_element_type=jnp.float32)
    ).astype(jnp.bfloat16)
    mixed = (
        w_depth[0][None, :, None] * hidden[:-2]
        + w_depth[1][None, :, None] * hidden[1:-1]
        + w_depth[2][None, :, None] * hidden[2:]
    ).astype(jnp.bfloat16)
    predicted_column = column_profiles.astype(jnp.float32) + jnp.einsum(
        "khm,hc->kcm", mixed, w_out, preferred_element_type=jnp.float32
    )
    grand_accumulation = taken_together(jnp.sum(predicted_column, axis=2), "mem")
    profile_average = grand_accumulation / members
    departure_from_average = predicted_column - profile_average[:, :, None]
    pobs = jnp.einsum("kcm,co->kom", departure_from_average, obs_op, precision=top)
    mobs = jnp.dot(profile_average, obs_op, precision=top)
    hits = (foot[:, :, None] == jnp.arange(col_dev, dtype=jnp.int32)[None, None, :]).astype(
        jnp.float32
    )
    counts = jnp.sum((foot >= 0).astype(jnp.float32), axis=1)
    onehot = jnp.sum(hits, axis=1) / counts[:, None]
    fpert = jnp.einsum("bk,kom->bom", onehot, pobs, precision=top)
    fmean = jnp.dot(onehot, mobs, precision=top)
    scale = 1.0 / math.sqrt(members - 1)
    spread = (rinv[:, :, None] * fpert * scale).astype(jnp.bfloat16)
    innov = (rinv * (obs - fmean)).astype(jnp.bfloat16)
    target = owner[:, 0]
    capacity = max(2, 2 * src_b // n_cols)
    owner_hits = (target[:, None] == jnp.arange(n_cols, dtype=jnp.int32)[None, :]).astype(jnp.int32)
    ranking = jnp.sum((jnp.cumsum(owner_hits, axis=0) - 1) * owner_hits, axis=1)
    slot = target * capacity + ranking
    placing = (slot[:, None] == jnp.arange(n_cols * capacity, dtype=jnp.int32)[None, :]).astype(
        jnp.bfloat16
    )
    send_spread = jnp.einsum(
        "bq,bom->qom", placing, spread, preferred_element_type=jnp.float32
    ).astype(jnp.bfloat16)
    send_innov = jnp.einsum("bq,bo->qo", placing, innov, preferred_element_type=jnp.float32).astype(
        jnp.bfloat16
    )
    held_spread, held_innov = in_one_piece((send_spread, send_innov), "cols", 0, 0, 2)
    held_factor = jnp.full((held_spread.shape[0],), inflation[0] * inflation[0], jnp.float32)
    quarter = held_spread.shape[0] // n_mem
    factor_grid = jnp.broadcast_to(held_factor[:, None, None], held_spread.shape)
    portion, factor_part = tuple(
        (
            part.astype(jnp.float32)
            for part in in_one_piece_2(
                (
                    held_spread.astype(jnp.float32).astype(jnp.bfloat16),
                    factor_grid.astype(jnp.bfloat16),
                ),
                "mem",
                0,
                2,
                1,
            )
        )
    )
    innov_part = lax.dynamic_slice_in_dim(held_innov, lax.axis_index("mem") * quarter, quarter, 0)
    weighted = portion * factor_part
    whole = jnp.einsum("qom,qoj->mj", weighted, portion, precision=top)
    vector = jnp.einsum("qom,qo->m", weighted, innov_part.astype(jnp.float32), precision=top)
    half = members // 2
    folded = jnp.tril(whole[half:, half:]) + jnp.tril(whole[:half, :half], -1).T
    lower_left, folded, diagonal, vec_all = together(
        (whole[half:, :half], folded, jnp.diagonal(whole[:half, :half]), vector), ("cols", "mem")
    )
    upper_left = jnp.triu(folded, 1).T + jnp.diag(diagonal)
    gram_low = jnp.concatenate(
        [
            jnp.concatenate([upper_left, jnp.zeros_like(upper_left)], axis=1),
            jnp.concatenate([lower_left, jnp.tril(folded)], axis=1),
        ],
        axis=0,
    )
    gram = jnp.eye(members, dtype=jnp.float32) + gram_low
    chol_inverse = factor_inverse(gram)
    weights = jnp.dot(chol_inverse.T, jnp.dot(chol_inverse, vec_all, precision=top), precision=top)
    first = lax.axis_index("mem") * mem_dev
    tinv_mine = lax.dynamic_slice_in_dim(chol_inverse, first, mem_dev, 0).T
    mix_w = (weights[:, None] * scale + tinv_mine).astype(jnp.bfloat16)
    pertb = departure_from_average.astype(jnp.bfloat16)
    moved = jnp.einsum(
        "kcm,mj->kcj", collect(pertb, "mem", 2), mix_w, preferred_element_type=jnp.float32
    )
    return (profile_average[:, :, None] + moved).astype(jnp.bfloat16)


def solution(mesh):
    placed = (
        P("cols", None, "mem"),
        P(),
        P(),
        P(),
        P(),
        P("cols", None),
        P("cols", None),
        P("cols", None),
        P("cols", None),
        P("cols"),
    )
    return jax.shard_map(
        body, mesh=mesh, in_specs=placed, out_specs=P("cols", None, "mem"), check_vma=False
    )
```

```python
import math

import jax
import jax.numpy as jnp
from jax import lax
from jax.experimental import pallas as pl
from jax.experimental.pallas import tpu as pltpu
from jax.sharding import PartitionSpec as P


def extended(block, sides, width):
    for axis, dim in sides:
        count = lax.axis_size(axis)
        forward = [(i, i + 1) for i in range(count - 1)]
        backward = [(target, source) for source, target in forward]
        low = lax.ppermute(
            lax.slice_in_dim(block, block.shape[dim] - width, None, axis=dim), axis, forward
        )
        high = lax.ppermute(lax.slice_in_dim(block, 0, width, axis=dim), axis, backward)
        block = jnp.concatenate([low, block, high], axis=dim)
    return block


def sent_to_all(shard, axis):
    peers = lax.axis_size(axis)
    return lax.all_to_all(
        jnp.broadcast_to(shard[None], (peers, *shard.shape)), axis, 0, 0, tiled=True
    )


def taken_together(shard, axis):
    everything = sent_to_all(shard, axis)
    return jnp.sum(everything, axis=0)


def in_one_piece(arrays, axis, split_dim, concat_dim, along):
    columns = [a.reshape(*a.shape[:along], -1) for a in arrays]
    both = jnp.concatenate(columns, axis=along)
    out, at, done = (
        lax.all_to_all(both, axis, split_axis=split_dim, concat_axis=concat_dim, tiled=True),
        0,
        [],
    )
    for a, column in zip(arrays, columns):
        section = out[..., at : at + column.shape[along]]
        done.append(section.reshape(*section.shape[:along], *a.shape[along:]))
        at += column.shape[along]
    return tuple(done)


def in_one_piece_2(arrays, axis, split_dim, concat_dim, along):
    ends, at = ([], 0)
    for a in arrays[:-1]:
        at += a.shape[along]
        ends.append(at)
    both = jnp.concatenate(arrays, axis=along)
    return tuple(
        jnp.split(
            lax.all_to_all(both, axis, split_axis=split_dim, concat_axis=concat_dim, tiled=True),
            ends,
            axis=along,
        )
    )


def together(arrays, axis):
    ravelled, at, done = (jnp.concatenate([a.reshape(-1) for a in arrays]), 0, [])
    subtotal = lax.psum(ravelled, axis)
    for a in arrays:
        done.append(subtotal[at : at + a.size].reshape(a.shape))
        at += a.size
    return tuple(done)


def summed_everywhere(arrays):
    flat = jnp.concatenate([a.reshape(-1) for a in arrays])
    peers = lax.axis_size("cols")
    size = flat.shape[0]
    width = -(-size // peers)
    flat = jnp.pad(flat, (0, width * peers - size))
    pieces = lax.all_to_all(flat.reshape(peers, width), "cols", 0, 0, tiled=True)
    mine = lax.psum(jnp.sum(pieces, axis=0), "mem")
    total, at, done = sent_to_all(mine, "cols").reshape(-1), 0, []
    for a in arrays:
        done.append(total[at : at + a.size].reshape(a.shape))
        at += a.size
    return tuple(done)


def joined_along(parts, dim):
    parts = jnp.moveaxis(parts, 0, dim)
    lengths = parts.shape
    return parts.reshape(*lengths[:dim], lengths[dim] * lengths[dim + 1], *lengths[dim + 2 :])


def collect(shard, axis, dim):
    return joined_along(sent_to_all(shard, axis), dim)


def _eliminate(a_ref, low_ref, inv_ref, m_ref):
    n = a_ref.shape[0]
    sub = lax.broadcasted_iota(jnp.int32, (n, 1), 0)
    lane = lax.broadcasted_iota(jnp.int32, (1, n), 1)
    rows = lax.broadcasted_iota(jnp.int32, (n, n), 0)
    cols = lax.broadcasted_iota(jnp.int32, (n, n), 1)
    m_ref[:, :n] = a_ref[...]
    m_ref[:, n:] = (rows == cols).astype(jnp.float32)

    def step(j, carry):
        row = m_ref[pl.ds(j, 1), :]
        whole = m_ref[...]
        column = jnp.sum(jnp.where(lane == j, whole[:, :n], 0.0), axis=1, keepdims=True)
        pivot = jnp.sum(jnp.where(lane == j, row[:, :n], 0.0), axis=1, keepdims=True)
        factor = jnp.where(sub > j, column / pivot, 0.0)
        m_ref[...] = whole - factor * row
        return carry

    lax.fori_loop(0, n, step, 0)
    whole = m_ref[...]
    diag = jnp.sum(jnp.where(rows == cols, whole[:, :n], 0.0), axis=1, keepdims=True)
    scale = 1.0 / jnp.sqrt(diag)
    low_ref[...] = jnp.where(rows <= cols, whole[:, :n] * scale, 0.0)
    inv_ref[...] = whole[:, n:] * scale


def factor_block(block):
    width = block.shape[0]
    symmetric = jnp.tril(block) + jnp.tril(block, -1).T
    square = jax.ShapeDtypeStruct((width, width), jnp.float32)
    upper, inverse = pl.pallas_call(
        _eliminate,
        out_shape=(square, square),
        in_specs=[pl.BlockSpec(memory_space=pltpu.VMEM)],
        out_specs=(pl.BlockSpec(memory_space=pltpu.VMEM), pl.BlockSpec(memory_space=pltpu.VMEM)),
        scratch_shapes=[pltpu.VMEM((width, 2 * width), jnp.float32)],
    )(symmetric)
    return upper.T, inverse


def factor_inverse(gram):
    top = lax.Precision.HIGHEST
    order = gram.shape[0]
    step_size = min(128, order)
    identity = jnp.eye(order, dtype=jnp.float32)
    chol = jnp.zeros((order, order), jnp.float32)
    chol_inverse = jnp.zeros((order, order), jnp.float32)
    for block_index in range(order // step_size):
        begin = block_index * step_size
        finish = begin + step_size
        panel = gram[begin:, begin:finish]
        if block_index > 0:
            panel = panel - jnp.dot(
                chol[begin:, :begin], chol[begin:finish, :begin].T, precision=top
            )
        diag_low, diag_inverse = factor_block(panel[:step_size])
        below = jnp.dot(panel[step_size:], diag_inverse.T, precision=top)
        chol = chol.at[begin:, begin:finish].set(jnp.concatenate([diag_low, below], axis=0))
        right_side = identity[begin:finish]
        if block_index > 0:
            right_side = right_side - jnp.dot(
                chol[begin:finish, :begin], chol_inverse[:begin], precision=top
            )
        chol_inverse = chol_inverse.at[begin:finish].set(
            jnp.dot(diag_inverse, right_side, precision=top)
        )
    return chol_inverse


def body(column_profiles, w_in, w_depth, w_out, obs_op, foot, owner, obs, rinv, inflation):
    top = lax.Precision.HIGHEST
    n_cols = lax.axis_size("cols")
    n_mem = lax.axis_size("mem")
    mem_dev = column_profiles.shape[2]
    members = mem_dev * n_mem
    src_b = foot.shape[0]
    col_dev = column_profiles.shape[0]
    widened = extended(column_profiles, (("cols", 0),), 1)
    hidden = jax.nn.gelu(
        jnp.einsum("kcm,ch->khm", widened, w_in, preferred_element_type=jnp.float32)
    ).astype(jnp.bfloat16)
    mixed = (
        w_depth[0][None, :, None] * hidden[:-2]
        + w_depth[1][None, :, None] * hidden[1:-1]
        + w_depth[2][None, :, None] * hidden[2:]
    ).astype(jnp.bfloat16)
    predicted_column = column_profiles.astype(jnp.float32) + jnp.einsum(
        "khm,hc->kcm", mixed, w_out, preferred_element_type=jnp.float32
    )
    grand_accumulation = taken_together(jnp.sum(predicted_column, axis=2), "mem")
    profile_average = grand_accumulation / members
    departure_from_average = predicted_column - profile_average[:, :, None]
    pobs = jnp.einsum("kcm,co->kom", departure_from_average, obs_op, precision=top)
    mobs = jnp.dot(profile_average, obs_op, precision=top)
    hits = (foot[:, :, None] == jnp.arange(col_dev, dtype=jnp.int32)[None, None, :]).astype(
        jnp.float32
    )
    counts = jnp.sum((foot >= 0).astype(jnp.float32), axis=1)
    onehot = jnp.sum(hits, axis=1) / counts[:, None]
    fpert = jnp.einsum("bk,kom->bom", onehot, pobs, precision=top)
    fmean = jnp.dot(onehot, mobs, precision=top)
    scale = 1.0 / math.sqrt(members - 1)
    spread = (rinv[:, :, None] * fpert * scale).astype(jnp.bfloat16)
    innov = (rinv * (obs - fmean)).astype(jnp.bfloat16)
    target = owner[:, 0]
    capacity = max(2, 2 * src_b // n_cols)
    owner_hits = (target[:, None] == jnp.arange(n_cols, dtype=jnp.int32)[None, :]).astype(jnp.int32)
    ranking = jnp.sum((jnp.cumsum(owner_hits, axis=0) - 1) * owner_hits, axis=1)
    slot = target * capacity + ranking
    placing = (slot[:, None] == jnp.arange(n_cols * capacity, dtype=jnp.int32)[None, :]).astype(
        jnp.bfloat16
    )
    send_spread = jnp.einsum(
        "bq,bom->qom", placing, spread, preferred_element_type=jnp.float32
    ).astype(jnp.bfloat16)
    send_innov = jnp.einsum("bq,bo->qo", placing, innov, preferred_element_type=jnp.float32).astype(
        jnp.bfloat16
    )
    held_spread, held_innov = in_one_piece((send_spread, send_innov), "cols", 0, 0, 2)
    held_factor = jnp.full((held_spread.shape[0],), inflation[0] * inflation[0], jnp.float32)
    quarter = held_spread.shape[0] // n_mem
    factor_grid = jnp.broadcast_to(held_factor[:, None, None], held_spread.shape)
    portion, factor_part = tuple(
        (
            part.astype(jnp.float32)
            for part in in_one_piece_2(
                (
                    held_spread.astype(jnp.float32).astype(jnp.bfloat16),
                    factor_grid.astype(jnp.bfloat16),
                ),
                "mem",
                0,
                2,
                1,
            )
        )
    )
    innov_part = lax.dynamic_slice_in_dim(held_innov, lax.axis_index("mem") * quarter, quarter, 0)
    weighted = portion * factor_part
    whole = jnp.einsum("qom,qoj->mj", weighted, portion, precision=top)
    vector = jnp.einsum("qom,qo->m", weighted, innov_part.astype(jnp.float32), precision=top)
    half = members // 2
    folded = jnp.tril(whole[half:, half:]) + jnp.tril(whole[:half, :half], -1).T
    lower_left, folded, diagonal, vec_all = summed_everywhere(
        (whole[half:, :half], folded, jnp.diagonal(whole[:half, :half]), vector)
    )
    upper_left = jnp.triu(folded, 1).T + jnp.diag(diagonal)
    gram_low = jnp.concatenate(
        [
            jnp.concatenate([upper_left, jnp.zeros_like(upper_left)], axis=1),
            jnp.concatenate([lower_left, jnp.tril(folded)], axis=1),
        ],
        axis=0,
    )
    gram = jnp.eye(members, dtype=jnp.float32) + gram_low
    chol_inverse = factor_inverse(gram)
    weights = jnp.dot(chol_inverse.T, jnp.dot(chol_inverse, vec_all, precision=top), precision=top)
    first = lax.axis_index("mem") * mem_dev
    tinv_mine = lax.dynamic_slice_in_dim(chol_inverse, first, mem_dev, 0).T
    mix_w = (weights[:, None] * scale + tinv_mine).astype(jnp.bfloat16)
    pertb = departure_from_average.astype(jnp.bfloat16)
    moved = jnp.einsum(
        "kcm,mj->kcj", collect(pertb, "mem", 2), mix_w, preferred_element_type=jnp.float32
    )
    return (profile_average[:, :, None] + moved).astype(jnp.bfloat16)


def solution(mesh):
    placed = (
        P("cols", None, "mem"),
        P(),
        P(),
        P(),
        P(),
        P("cols", None),
        P("cols", None),
        P("cols", None),
        P("cols", None),
        P("cols"),
    )
    return jax.shard_map(
        body, mesh=mesh, in_specs=placed, out_specs=P("cols", None, "mem"), check_vma=False
    )
```

```python
import math

import jax
import jax.numpy as jnp
from jax import lax
from jax.experimental import pallas as pl
from jax.experimental.pallas import tpu as pltpu
from jax.sharding import PartitionSpec as P


def extended(block, sides, width):
    for axis, dim in sides:
        count = lax.axis_size(axis)
        forward = [(i, i + 1) for i in range(count - 1)]
        backward = [(target, source) for source, target in forward]
        low = lax.ppermute(
            lax.slice_in_dim(block, block.shape[dim] - width, None, axis=dim), axis, forward
        )
        high = lax.ppermute(lax.slice_in_dim(block, 0, width, axis=dim), axis, backward)
        block = jnp.concatenate([low, block, high], axis=dim)
    return block


def sent_to_all(shard, axis):
    peers = lax.axis_size(axis)
    return lax.all_to_all(
        jnp.broadcast_to(shard[None], (peers, *shard.shape)), axis, 0, 0, tiled=True
    )


def taken_together(shard, axis):
    everything = sent_to_all(shard, axis)
    return jnp.sum(everything, axis=0)


def in_one_piece(arrays, axis, split_dim, concat_dim, along):
    columns = [a.reshape(*a.shape[:along], -1) for a in arrays]
    both = jnp.concatenate(columns, axis=along)
    out, at, done = (
        lax.all_to_all(both, axis, split_axis=split_dim, concat_axis=concat_dim, tiled=True),
        0,
        [],
    )
    for a, column in zip(arrays, columns):
        section = out[..., at : at + column.shape[along]]
        done.append(section.reshape(*section.shape[:along], *a.shape[along:]))
        at += column.shape[along]
    return tuple(done)


def in_one_piece_2(arrays, axis, split_dim, concat_dim, along):
    ends, at = ([], 0)
    for a in arrays[:-1]:
        at += a.shape[along]
        ends.append(at)
    both = jnp.concatenate(arrays, axis=along)
    return tuple(
        jnp.split(
            lax.all_to_all(both, axis, split_axis=split_dim, concat_axis=concat_dim, tiled=True),
            ends,
            axis=along,
        )
    )


def together(arrays, axis):
    ravelled, at, done = (jnp.concatenate([a.reshape(-1) for a in arrays]), 0, [])
    subtotal = lax.psum(ravelled, axis)
    for a in arrays:
        done.append(subtotal[at : at + a.size].reshape(a.shape))
        at += a.size
    return tuple(done)


def summed_everywhere(arrays):
    flat = jnp.concatenate([a.reshape(-1) for a in arrays])
    peers = lax.axis_size("cols")
    size = flat.shape[0]
    width = -(-size // peers)
    flat = jnp.pad(flat, (0, width * peers - size))
    pieces = lax.all_to_all(flat.reshape(peers, width), "cols", 0, 0, tiled=True)
    mine = lax.psum(jnp.sum(pieces, axis=0), "mem")
    total, at, done = sent_to_all(mine, "cols").reshape(-1), 0, []
    for a in arrays:
        done.append(total[at : at + a.size].reshape(a.shape))
        at += a.size
    return tuple(done)


def joined_along(parts, dim):
    parts = jnp.moveaxis(parts, 0, dim)
    lengths = parts.shape
    return parts.reshape(*lengths[:dim], lengths[dim] * lengths[dim + 1], *lengths[dim + 2 :])


def collect(shard, axis, dim):
    return joined_along(sent_to_all(shard, axis), dim)


def _eliminate(a_ref, low_ref, inv_ref, m_ref):
    n = a_ref.shape[0]
    sub = lax.broadcasted_iota(jnp.int32, (n, 1), 0)
    lane = lax.broadcasted_iota(jnp.int32, (1, n), 1)
    rows = lax.broadcasted_iota(jnp.int32, (n, n), 0)
    cols = lax.broadcasted_iota(jnp.int32, (n, n), 1)
    m_ref[:, :n] = a_ref[...]
    m_ref[:, n:] = (rows == cols).astype(jnp.float32)

    def step(j, carry):
        row = m_ref[pl.ds(j, 1), :]
        whole = m_ref[...]
        column = jnp.sum(jnp.where(lane == j, whole[:, :n], 0.0), axis=1, keepdims=True)
        pivot = jnp.sum(jnp.where(lane == j, row[:, :n], 0.0), axis=1, keepdims=True)
        factor = jnp.where(sub > j, column / pivot, 0.0)
        m_ref[...] = whole - factor * row
        return carry

    lax.fori_loop(0, n, step, 0)
    whole = m_ref[...]
    diag = jnp.sum(jnp.where(rows == cols, whole[:, :n], 0.0), axis=1, keepdims=True)
    scale = 1.0 / jnp.sqrt(diag)
    low_ref[...] = jnp.where(rows <= cols, whole[:, :n] * scale, 0.0)
    inv_ref[...] = whole[:, n:] * scale


def factor_block(block):
    width = block.shape[0]
    symmetric = jnp.tril(block) + jnp.tril(block, -1).T
    square = jax.ShapeDtypeStruct((width, width), jnp.float32)
    upper, inverse = pl.pallas_call(
        _eliminate,
        out_shape=(square, square),
        in_specs=[pl.BlockSpec(memory_space=pltpu.VMEM)],
        out_specs=(pl.BlockSpec(memory_space=pltpu.VMEM), pl.BlockSpec(memory_space=pltpu.VMEM)),
        scratch_shapes=[pltpu.VMEM((width, 2 * width), jnp.float32)],
    )(symmetric)
    return upper.T, inverse


def factor_inverse(gram):
    top = lax.Precision.HIGHEST
    order = gram.shape[0]
    step_size = min(128, order)
    identity = jnp.eye(order, dtype=jnp.float32)
    chol = jnp.zeros((order, order), jnp.float32)
    chol_inverse = jnp.zeros((order, order), jnp.float32)
    for block_index in range(order // step_size):
        begin = block_index * step_size
        finish = begin + step_size
        panel = gram[begin:, begin:finish]
        if block_index > 0:
            panel = panel - jnp.dot(
                chol[begin:, :begin], chol[begin:finish, :begin].T, precision=top
            )
        diag_low, diag_inverse = factor_block(panel[:step_size])
        below = jnp.dot(panel[step_size:], diag_inverse.T, precision=top)
        chol = chol.at[begin:, begin:finish].set(jnp.concatenate([diag_low, below], axis=0))
        right_side = identity[begin:finish]
        if block_index > 0:
            right_side = right_side - jnp.dot(
                chol[begin:finish, :begin], chol_inverse[:begin], precision=top
            )
        chol_inverse = chol_inverse.at[begin:finish].set(
            jnp.dot(diag_inverse, right_side, precision=top)
        )
    return chol_inverse


def body(column_profiles, w_in, w_depth, w_out, obs_op, foot, owner, obs, rinv, inflation):
    top = lax.Precision.HIGHEST
    n_cols = lax.axis_size("cols")
    n_mem = lax.axis_size("mem")
    mem_dev = column_profiles.shape[2]
    members = mem_dev * n_mem
    src_b = foot.shape[0]
    col_dev = column_profiles.shape[0]
    widened = extended(column_profiles, (("cols", 0),), 1)
    hidden = jax.nn.gelu(
        jnp.einsum("kcm,ch->khm", widened, w_in, preferred_element_type=jnp.float32)
    ).astype(jnp.bfloat16)
    mixed = (
        w_depth[0][None, :, None] * hidden[:-2]
        + w_depth[1][None, :, None] * hidden[1:-1]
        + w_depth[2][None, :, None] * hidden[2:]
    ).astype(jnp.bfloat16)
    predicted_column = column_profiles.astype(jnp.float32) + jnp.einsum(
        "khm,hc->kcm", mixed, w_out, preferred_element_type=jnp.float32
    )
    grand_accumulation = taken_together(jnp.sum(predicted_column, axis=2), "mem")
    profile_average = grand_accumulation / members
    departure_from_average = predicted_column - profile_average[:, :, None]
    pobs = jnp.einsum("kcm,co->kom", departure_from_average, obs_op, precision=top)
    mobs = jnp.dot(profile_average, obs_op, precision=top)
    hits = (foot[:, :, None] == jnp.arange(col_dev, dtype=jnp.int32)[None, None, :]).astype(
        jnp.float32
    )
    counts = jnp.sum((foot >= 0).astype(jnp.float32), axis=1)
    onehot = jnp.sum(hits, axis=1) / counts[:, None]
    fpert = jnp.einsum("bk,kom->bom", onehot, pobs, precision=top)
    fmean = jnp.dot(onehot, mobs, precision=top)
    scale = 1.0 / math.sqrt(members - 1)
    spread = (rinv[:, :, None] * fpert * scale).astype(jnp.bfloat16)
    innov = (rinv * (obs - fmean)).astype(jnp.bfloat16)
    every_inflation = sent_to_all(inflation, "cols").reshape(-1)
    factor = every_inflation[owner[:, 0]] ** 2
    quarter = src_b // n_mem
    first_batch = lax.axis_index("mem") * quarter
    portion = lax.all_to_all(spread, "mem", 0, 2, tiled=True).astype(jnp.float32)
    innov_part = lax.dynamic_slice_in_dim(innov, first_batch, quarter, 0)
    factor_part = lax.dynamic_slice_in_dim(factor, first_batch, quarter, 0)
    weighted = portion * factor_part[:, None, None]
    whole = jnp.einsum("qom,qoj->mj", weighted, portion, precision=top)
    vector = jnp.einsum("qom,qo->m", weighted, innov_part.astype(jnp.float32), precision=top)
    half = members // 2
    folded = jnp.tril(whole[half:, half:]) + jnp.tril(whole[:half, :half], -1).T
    lower_left, folded, diagonal, vec_all = summed_everywhere(
        (whole[half:, :half], folded, jnp.diagonal(whole[:half, :half]), vector)
    )
    upper_left = jnp.triu(folded, 1).T + jnp.diag(diagonal)
    gram_low = jnp.concatenate(
        [
            jnp.concatenate([upper_left, jnp.zeros_like(upper_left)], axis=1),
            jnp.concatenate([lower_left, jnp.tril(folded)], axis=1),
        ],
        axis=0,
    )
    gram = jnp.eye(members, dtype=jnp.float32) + gram_low
    chol_inverse = factor_inverse(gram)
    weights = jnp.dot(chol_inverse.T, jnp.dot(chol_inverse, vec_all, precision=top), precision=top)
    first = lax.axis_index("mem") * mem_dev
    tinv_mine = lax.dynamic_slice_in_dim(chol_inverse, first, mem_dev, 0).T
    mix_w = (weights[:, None] * scale + tinv_mine).astype(jnp.bfloat16)
    pertb = departure_from_average.astype(jnp.bfloat16)
    moved = jnp.einsum(
        "kcm,mj->kcj", collect(pertb, "mem", 2), mix_w, preferred_element_type=jnp.float32
    )
    return (profile_average[:, :, None] + moved).astype(jnp.bfloat16)


def solution(mesh):
    placed = (
        P("cols", None, "mem"),
        P(),
        P(),
        P(),
        P(),
        P("cols", None),
        P("cols", None),
        P("cols", None),
        P("cols", None),
        P("cols"),
    )
    return jax.shard_map(
        body, mesh=mesh, in_specs=placed, out_specs=P("cols", None, "mem"), check_vma=False
    )
```

```python
import math

import jax
import jax.numpy as jnp
from jax import lax
from jax.experimental import pallas as pl
from jax.experimental.pallas import tpu as pltpu
from jax.sharding import PartitionSpec as P


def extended(block, sides, width):
    for axis, dim in sides:
        count = lax.axis_size(axis)
        forward = [(i, i + 1) for i in range(count - 1)]
        backward = [(target, source) for source, target in forward]
        low = lax.ppermute(
            lax.slice_in_dim(block, block.shape[dim] - width, None, axis=dim), axis, forward
        )
        high = lax.ppermute(lax.slice_in_dim(block, 0, width, axis=dim), axis, backward)
        block = jnp.concatenate([low, block, high], axis=dim)
    return block


def sent_to_all(shard, axis):
    peers = lax.axis_size(axis)
    return lax.all_to_all(
        jnp.broadcast_to(shard[None], (peers, *shard.shape)), axis, 0, 0, tiled=True
    )


def taken_together(shard, axis):
    everything = sent_to_all(shard, axis)
    return jnp.sum(everything, axis=0)


def in_one_piece(arrays, axis, split_dim, concat_dim, along):
    columns = [a.reshape(*a.shape[:along], -1) for a in arrays]
    both = jnp.concatenate(columns, axis=along)
    out, at, done = (
        lax.all_to_all(both, axis, split_axis=split_dim, concat_axis=concat_dim, tiled=True),
        0,
        [],
    )
    for a, column in zip(arrays, columns):
        section = out[..., at : at + column.shape[along]]
        done.append(section.reshape(*section.shape[:along], *a.shape[along:]))
        at += column.shape[along]
    return tuple(done)


def in_one_piece_2(arrays, axis, split_dim, concat_dim, along):
    ends, at = ([], 0)
    for a in arrays[:-1]:
        at += a.shape[along]
        ends.append(at)
    both = jnp.concatenate(arrays, axis=along)
    return tuple(
        jnp.split(
            lax.all_to_all(both, axis, split_axis=split_dim, concat_axis=concat_dim, tiled=True),
            ends,
            axis=along,
        )
    )


def together(arrays, axis):
    ravelled, at, done = (jnp.concatenate([a.reshape(-1) for a in arrays]), 0, [])
    subtotal = lax.psum(ravelled, axis)
    for a in arrays:
        done.append(subtotal[at : at + a.size].reshape(a.shape))
        at += a.size
    return tuple(done)


def summed_everywhere(arrays):
    flat = jnp.concatenate([a.reshape(-1) for a in arrays])
    n_cols, n_mem = lax.axis_size("cols"), lax.axis_size("mem")
    size = flat.shape[0]
    width = -(-size // (n_cols * n_mem))
    flat = jnp.pad(flat, (0, width * n_cols * n_mem - size))
    part = lax.all_to_all(flat.reshape(n_mem, n_cols * width), "mem", 0, 0, tiled=True)
    pieces = lax.all_to_all(jnp.sum(part, axis=0).reshape(n_cols, width), "cols", 0, 0, tiled=True)
    mine = jnp.sum(pieces, axis=0)
    back = sent_to_all(mine, "cols").reshape(-1)
    total, at, done = sent_to_all(back, "mem").reshape(-1), 0, []
    for a in arrays:
        done.append(total[at : at + a.size].reshape(a.shape))
        at += a.size
    return tuple(done)


def joined_along(parts, dim):
    parts = jnp.moveaxis(parts, 0, dim)
    lengths = parts.shape
    return parts.reshape(*lengths[:dim], lengths[dim] * lengths[dim + 1], *lengths[dim + 2 :])


def collect(shard, axis, dim):
    return joined_along(sent_to_all(shard, axis), dim)


def _eliminate(a_ref, low_ref, inv_ref, m_ref):
    n = a_ref.shape[0]
    sub = lax.broadcasted_iota(jnp.int32, (n, 1), 0)
    lane = lax.broadcasted_iota(jnp.int32, (1, n), 1)
    rows = lax.broadcasted_iota(jnp.int32, (n, n), 0)
    cols = lax.broadcasted_iota(jnp.int32, (n, n), 1)
    m_ref[:, :n] = a_ref[...]
    m_ref[:, n:] = (rows == cols).astype(jnp.float32)

    def step(j, carry):
        row = m_ref[pl.ds(j, 1), :]
        whole = m_ref[...]
        column = jnp.sum(jnp.where(lane == j, whole[:, :n], 0.0), axis=1, keepdims=True)
        pivot = jnp.sum(jnp.where(lane == j, row[:, :n], 0.0), axis=1, keepdims=True)
        factor = jnp.where(sub > j, column / pivot, 0.0)
        m_ref[...] = whole - factor * row
        return carry

    lax.fori_loop(0, n, step, 0)
    whole = m_ref[...]
    diag = jnp.sum(jnp.where(rows == cols, whole[:, :n], 0.0), axis=1, keepdims=True)
    scale = 1.0 / jnp.sqrt(diag)
    low_ref[...] = jnp.where(rows <= cols, whole[:, :n] * scale, 0.0)
    inv_ref[...] = whole[:, n:] * scale


def factor_block(block):
    width = block.shape[0]
    symmetric = jnp.tril(block) + jnp.tril(block, -1).T
    square = jax.ShapeDtypeStruct((width, width), jnp.float32)
    upper, inverse = pl.pallas_call(
        _eliminate,
        out_shape=(square, square),
        in_specs=[pl.BlockSpec(memory_space=pltpu.VMEM)],
        out_specs=(pl.BlockSpec(memory_space=pltpu.VMEM), pl.BlockSpec(memory_space=pltpu.VMEM)),
        scratch_shapes=[pltpu.VMEM((width, 2 * width), jnp.float32)],
    )(symmetric)
    return upper.T, inverse


def factor_inverse(gram):
    top = lax.Precision.HIGHEST
    order = gram.shape[0]
    step_size = min(128, order)
    identity = jnp.eye(order, dtype=jnp.float32)
    chol = jnp.zeros((order, order), jnp.float32)
    chol_inverse = jnp.zeros((order, order), jnp.float32)
    for block_index in range(order // step_size):
        begin = block_index * step_size
        finish = begin + step_size
        panel = gram[begin:, begin:finish]
        if block_index > 0:
            panel = panel - jnp.dot(
                chol[begin:, :begin], chol[begin:finish, :begin].T, precision=top
            )
        diag_low, diag_inverse = factor_block(panel[:step_size])
        below = jnp.dot(panel[step_size:], diag_inverse.T, precision=top)
        chol = chol.at[begin:, begin:finish].set(jnp.concatenate([diag_low, below], axis=0))
        right_side = identity[begin:finish]
        if block_index > 0:
            right_side = right_side - jnp.dot(
                chol[begin:finish, :begin], chol_inverse[:begin], precision=top
            )
        chol_inverse = chol_inverse.at[begin:finish].set(
            jnp.dot(diag_inverse, right_side, precision=top)
        )
    return chol_inverse


def body(column_profiles, w_in, w_depth, w_out, obs_op, foot, owner, obs, rinv, inflation):
    top = lax.Precision.HIGHEST
    n_cols = lax.axis_size("cols")
    n_mem = lax.axis_size("mem")
    mem_dev = column_profiles.shape[2]
    members = mem_dev * n_mem
    src_b = foot.shape[0]
    col_dev = column_profiles.shape[0]
    widened = extended(column_profiles, (("cols", 0),), 1)
    hidden = jax.nn.gelu(
        jnp.einsum("kcm,ch->khm", widened, w_in, preferred_element_type=jnp.float32)
    ).astype(jnp.bfloat16)
    mixed = (
        w_depth[0][None, :, None] * hidden[:-2]
        + w_depth[1][None, :, None] * hidden[1:-1]
        + w_depth[2][None, :, None] * hidden[2:]
    ).astype(jnp.bfloat16)
    predicted_column = column_profiles.astype(jnp.float32) + jnp.einsum(
        "khm,hc->kcm", mixed, w_out, preferred_element_type=jnp.float32
    )
    grand_accumulation = taken_together(jnp.sum(predicted_column, axis=2), "mem")
    profile_average = grand_accumulation / members
    departure_from_average = predicted_column - profile_average[:, :, None]
    pobs = jnp.einsum("kcm,co->kom", departure_from_average, obs_op, precision=top)
    mobs = jnp.dot(profile_average, obs_op, precision=top)
    hits = (foot[:, :, None] == jnp.arange(col_dev, dtype=jnp.int32)[None, None, :]).astype(
        jnp.float32
    )
    counts = jnp.sum((foot >= 0).astype(jnp.float32), axis=1)
    onehot = jnp.sum(hits, axis=1) / counts[:, None]
    fpert = jnp.einsum("bk,kom->bom", onehot, pobs, precision=top)
    fmean = jnp.dot(onehot, mobs, precision=top)
    scale = 1.0 / math.sqrt(members - 1)
    spread = (rinv[:, :, None] * fpert * scale).astype(jnp.bfloat16)
    innov = (rinv * (obs - fmean)).astype(jnp.bfloat16)
    every_inflation = sent_to_all(inflation, "cols").reshape(-1)
    factor = every_inflation[owner[:, 0]] ** 2
    quarter = src_b // n_mem
    first_batch = lax.axis_index("mem") * quarter
    portion = lax.all_to_all(spread, "mem", 0, 2, tiled=True).astype(jnp.float32)
    innov_part = lax.dynamic_slice_in_dim(innov, first_batch, quarter, 0)
    factor_part = lax.dynamic_slice_in_dim(factor, first_batch, quarter, 0)
    weighted = portion * factor_part[:, None, None]
    whole = jnp.einsum("qom,qoj->mj", weighted, portion, precision=top)
    vector = jnp.einsum("qom,qo->m", weighted, innov_part.astype(jnp.float32), precision=top)
    half = members // 2
    folded = jnp.tril(whole[half:, half:]) + jnp.tril(whole[:half, :half], -1).T
    lower_left, folded, diagonal, vec_all = summed_everywhere(
        (whole[half:, :half], folded, jnp.diagonal(whole[:half, :half]), vector)
    )
    upper_left = jnp.triu(folded, 1).T + jnp.diag(diagonal)
    gram_low = jnp.concatenate(
        [
            jnp.concatenate([upper_left, jnp.zeros_like(upper_left)], axis=1),
            jnp.concatenate([lower_left, jnp.tril(folded)], axis=1),
        ],
        axis=0,
    )
    gram = jnp.eye(members, dtype=jnp.float32) + gram_low
    chol_inverse = factor_inverse(gram)
    weights = jnp.dot(chol_inverse.T, jnp.dot(chol_inverse, vec_all, precision=top), precision=top)
    first = lax.axis_index("mem") * mem_dev
    tinv_mine = lax.dynamic_slice_in_dim(chol_inverse, first, mem_dev, 0).T
    mix_w = (weights[:, None] * scale + tinv_mine).astype(jnp.bfloat16)
    pertb = departure_from_average.astype(jnp.bfloat16)
    moved = jnp.einsum(
        "kcm,mj->kcj", collect(pertb, "mem", 2), mix_w, preferred_element_type=jnp.float32
    )
    return (profile_average[:, :, None] + moved).astype(jnp.bfloat16)


def solution(mesh):
    placed = (
        P("cols", None, "mem"),
        P(),
        P(),
        P(),
        P(),
        P("cols", None),
        P("cols", None),
        P("cols", None),
        P("cols", None),
        P("cols"),
    )
    return jax.shard_map(
        body, mesh=mesh, in_specs=placed, out_specs=P("cols", None, "mem"), check_vma=False
    )
```

```python
import math

import jax
import jax.numpy as jnp
from jax import lax
from jax.experimental import pallas as pl
from jax.experimental.pallas import tpu as pltpu
from jax.sharding import PartitionSpec as P


def extended(block, sides, width):
    for axis, dim in sides:
        count = lax.axis_size(axis)
        forward = [(i, i + 1) for i in range(count - 1)]
        backward = [(target, source) for source, target in forward]
        low = lax.ppermute(
            lax.slice_in_dim(block, block.shape[dim] - width, None, axis=dim), axis, forward
        )
        high = lax.ppermute(lax.slice_in_dim(block, 0, width, axis=dim), axis, backward)
        block = jnp.concatenate([low, block, high], axis=dim)
    return block


def sent_to_all(shard, axis):
    peers = lax.axis_size(axis)
    return lax.all_to_all(
        jnp.broadcast_to(shard[None], (peers, *shard.shape)), axis, 0, 0, tiled=True
    )


def taken_together(shard, axis):
    everything = sent_to_all(shard, axis)
    return jnp.sum(everything, axis=0)


def in_one_piece(arrays, axis, split_dim, concat_dim, along):
    columns = [a.reshape(*a.shape[:along], -1) for a in arrays]
    both = jnp.concatenate(columns, axis=along)
    out, at, done = (
        lax.all_to_all(both, axis, split_axis=split_dim, concat_axis=concat_dim, tiled=True),
        0,
        [],
    )
    for a, column in zip(arrays, columns):
        section = out[..., at : at + column.shape[along]]
        done.append(section.reshape(*section.shape[:along], *a.shape[along:]))
        at += column.shape[along]
    return tuple(done)


def in_one_piece_2(arrays, axis, split_dim, concat_dim, along):
    ends, at = ([], 0)
    for a in arrays[:-1]:
        at += a.shape[along]
        ends.append(at)
    both = jnp.concatenate(arrays, axis=along)
    return tuple(
        jnp.split(
            lax.all_to_all(both, axis, split_axis=split_dim, concat_axis=concat_dim, tiled=True),
            ends,
            axis=along,
        )
    )


def together(arrays, axis):
    ravelled, at, done = (jnp.concatenate([a.reshape(-1) for a in arrays]), 0, [])
    subtotal = lax.psum(ravelled, axis)
    for a in arrays:
        done.append(subtotal[at : at + a.size].reshape(a.shape))
        at += a.size
    return tuple(done)


def summed_everywhere(arrays):
    flat = jnp.concatenate([a.reshape(-1) for a in arrays])
    n_cols, n_mem = lax.axis_size("cols"), lax.axis_size("mem")
    size = flat.shape[0]
    width = -(-size // (n_cols * n_mem))
    flat = jnp.pad(flat, (0, width * n_cols * n_mem - size))
    part = lax.all_to_all(flat.reshape(n_mem, n_cols * width), "mem", 0, 0, tiled=True)
    pieces = lax.all_to_all(jnp.sum(part, axis=0).reshape(n_cols, width), "cols", 0, 0, tiled=True)
    mine = jnp.sum(pieces, axis=0)
    back = sent_to_all(mine, "cols").reshape(-1)
    total, at, done = sent_to_all(back, "mem").reshape(-1), 0, []
    for a in arrays:
        done.append(total[at : at + a.size].reshape(a.shape))
        at += a.size
    return tuple(done)


def joined_along(parts, dim):
    parts = jnp.moveaxis(parts, 0, dim)
    lengths = parts.shape
    return parts.reshape(*lengths[:dim], lengths[dim] * lengths[dim + 1], *lengths[dim + 2 :])


def collect(shard, axis, dim):
    return joined_along(sent_to_all(shard, axis), dim)


def _eliminate(a_ref, low_ref, inv_ref, m_ref):
    n = a_ref.shape[0]
    sub = lax.broadcasted_iota(jnp.int32, (n, 1), 0)
    lane = lax.broadcasted_iota(jnp.int32, (1, n), 1)
    rows = lax.broadcasted_iota(jnp.int32, (n, n), 0)
    cols = lax.broadcasted_iota(jnp.int32, (n, n), 1)
    m_ref[:, :n] = a_ref[...]
    m_ref[:, n:] = (rows == cols).astype(jnp.float32)

    def step(j, carry):
        row = m_ref[pl.ds(j, 1), :]
        whole = m_ref[...]
        column = jnp.sum(jnp.where(lane == j, whole[:, :n], 0.0), axis=1, keepdims=True)
        pivot = jnp.sum(jnp.where(lane == j, row[:, :n], 0.0), axis=1, keepdims=True)
        factor = jnp.where(sub > j, column / pivot, 0.0)
        m_ref[...] = whole - factor * row
        return carry

    lax.fori_loop(0, n, step, 0)
    whole = m_ref[...]
    diag = jnp.sum(jnp.where(rows == cols, whole[:, :n], 0.0), axis=1, keepdims=True)
    scale = 1.0 / jnp.sqrt(diag)
    low_ref[...] = jnp.where(rows <= cols, whole[:, :n] * scale, 0.0)
    inv_ref[...] = whole[:, n:] * scale


def factor_block(block):
    width = block.shape[0]
    symmetric = jnp.tril(block) + jnp.tril(block, -1).T
    square = jax.ShapeDtypeStruct((width, width), jnp.float32)
    upper, inverse = pl.pallas_call(
        _eliminate,
        out_shape=(square, square),
        in_specs=[pl.BlockSpec(memory_space=pltpu.VMEM)],
        out_specs=(pl.BlockSpec(memory_space=pltpu.VMEM), pl.BlockSpec(memory_space=pltpu.VMEM)),
        scratch_shapes=[pltpu.VMEM((width, 2 * width), jnp.float32)],
    )(symmetric)
    return upper.T, inverse


def factor_inverse(gram):
    top = lax.Precision.HIGHEST
    order = gram.shape[0]
    step_size = min(128, order)
    identity = jnp.eye(order, dtype=jnp.float32)
    chol = jnp.zeros((order, order), jnp.float32)
    chol_inverse = jnp.zeros((order, order), jnp.float32)
    for block_index in range(order // step_size):
        begin = block_index * step_size
        finish = begin + step_size
        panel = gram[begin:, begin:finish]
        if block_index > 0:
            panel = panel - jnp.dot(
                chol[begin:, :begin], chol[begin:finish, :begin].T, precision=top
            )
        diag_low, diag_inverse = factor_block(panel[:step_size])
        below = jnp.dot(panel[step_size:], diag_inverse.T, precision=top)
        chol = chol.at[begin:, begin:finish].set(jnp.concatenate([diag_low, below], axis=0))
        right_side = identity[begin:finish]
        if block_index > 0:
            right_side = right_side - jnp.dot(
                chol[begin:finish, :begin], chol_inverse[:begin], precision=top
            )
        chol_inverse = chol_inverse.at[begin:finish].set(
            jnp.dot(diag_inverse, right_side, precision=top)
        )
    return chol_inverse


def body(column_profiles, w_in, w_depth, w_out, obs_op, foot, owner, obs, rinv, inflation):
    top = lax.Precision.HIGHEST
    n_cols = lax.axis_size("cols")
    n_mem = lax.axis_size("mem")
    mem_dev = column_profiles.shape[2]
    members = mem_dev * n_mem
    src_b = foot.shape[0]
    col_dev = column_profiles.shape[0]
    widened = extended(column_profiles, (("cols", 0),), 1)
    hidden = jax.nn.gelu(
        jnp.einsum("kcm,ch->khm", widened, w_in, preferred_element_type=jnp.float32)
    ).astype(jnp.bfloat16)
    mixed = (
        w_depth[0][None, :, None] * hidden[:-2]
        + w_depth[1][None, :, None] * hidden[1:-1]
        + w_depth[2][None, :, None] * hidden[2:]
    ).astype(jnp.bfloat16)
    predicted_column = column_profiles.astype(jnp.float32) + jnp.einsum(
        "khm,hc->kcm", mixed, w_out, preferred_element_type=jnp.float32
    )
    grand_accumulation = taken_together(jnp.sum(predicted_column, axis=2), "mem")
    profile_average = grand_accumulation / members
    departure_from_average = predicted_column - profile_average[:, :, None]
    pobs = jnp.einsum("kcm,co->kom", departure_from_average, obs_op, precision=top)
    mobs = jnp.dot(profile_average, obs_op, precision=top)
    hits = (foot[:, :, None] == jnp.arange(col_dev, dtype=jnp.int32)[None, None, :]).astype(
        jnp.float32
    )
    counts = jnp.sum((foot >= 0).astype(jnp.float32), axis=1)
    onehot = jnp.sum(hits, axis=1) / counts[:, None]
    fpert = jnp.einsum("bk,kom->bom", onehot, pobs, precision=top)
    fmean = jnp.dot(onehot, mobs, precision=top)
    scale = 1.0 / math.sqrt(members - 1)
    spread = (rinv[:, :, None] * fpert * scale).astype(jnp.bfloat16)
    innov = (rinv * (obs - fmean)).astype(jnp.bfloat16)
    every_inflation = sent_to_all(inflation, "cols").reshape(-1)
    factor = every_inflation[owner[:, 0]] ** 2
    quarter = src_b // n_mem
    first_batch = lax.axis_index("mem") * quarter
    pertb = departure_from_average.astype(jnp.bfloat16)
    own = pertb.shape[0] * pertb.shape[1]
    outgoing = jnp.concatenate(
        [
            jnp.broadcast_to(pertb.reshape(1, own, mem_dev), (n_mem, own, mem_dev)),
            spread.reshape(n_mem, -1, mem_dev),
        ],
        axis=1,
    )
    incoming = lax.all_to_all(outgoing, "mem", 0, 0, tiled=True)
    every_pertb = joined_along(incoming[:, :own].reshape(n_mem, *pertb.shape), 2)
    portion = joined_along(
        incoming[:, own:].reshape(n_mem, quarter, *spread.shape[1:]), 2
    ).astype(jnp.float32)
    innov_part = lax.dynamic_slice_in_dim(innov, first_batch, quarter, 0)
    factor_part = lax.dynamic_slice_in_dim(factor, first_batch, quarter, 0)
    weighted = portion * factor_part[:, None, None]
    whole = jnp.einsum("qom,qoj->mj", weighted, portion, precision=top)
    vector = jnp.einsum("qom,qo->m", weighted, innov_part.astype(jnp.float32), precision=top)
    half = members // 2
    folded = jnp.tril(whole[half:, half:]) + jnp.tril(whole[:half, :half], -1).T
    lower_left, folded, diagonal, vec_all = summed_everywhere(
        (whole[half:, :half], folded, jnp.diagonal(whole[:half, :half]), vector)
    )
    upper_left = jnp.triu(folded, 1).T + jnp.diag(diagonal)
    gram_low = jnp.concatenate(
        [
            jnp.concatenate([upper_left, jnp.zeros_like(upper_left)], axis=1),
            jnp.concatenate([lower_left, jnp.tril(folded)], axis=1),
        ],
        axis=0,
    )
    gram = jnp.eye(members, dtype=jnp.float32) + gram_low
    chol_inverse = factor_inverse(gram)
    weights = jnp.dot(chol_inverse.T, jnp.dot(chol_inverse, vec_all, precision=top), precision=top)
    first = lax.axis_index("mem") * mem_dev
    tinv_mine = lax.dynamic_slice_in_dim(chol_inverse, first, mem_dev, 0).T
    mix_w = (weights[:, None] * scale + tinv_mine).astype(jnp.bfloat16)
    moved = jnp.einsum("kcm,mj->kcj", every_pertb, mix_w, preferred_element_type=jnp.float32)
    return (profile_average[:, :, None] + moved).astype(jnp.bfloat16)


def solution(mesh):
    placed = (
        P("cols", None, "mem"),
        P(),
        P(),
        P(),
        P(),
        P("cols", None),
        P("cols", None),
        P("cols", None),
        P("cols", None),
        P("cols"),
    )
    return jax.shard_map(
        body, mesh=mesh, in_specs=placed, out_specs=P("cols", None, "mem"), check_vma=False
    )
```

```python
import math

import jax
import jax.numpy as jnp
from jax import lax
from jax.experimental import pallas as pl
from jax.experimental.pallas import tpu as pltpu
from jax.sharding import PartitionSpec as P


def extended(block, sides, width):
    for axis, dim in sides:
        count = lax.axis_size(axis)
        forward = [(i, i + 1) for i in range(count - 1)]
        backward = [(target, source) for source, target in forward]
        low = lax.ppermute(
            lax.slice_in_dim(block, block.shape[dim] - width, None, axis=dim), axis, forward
        )
        high = lax.ppermute(lax.slice_in_dim(block, 0, width, axis=dim), axis, backward)
        block = jnp.concatenate([low, block, high], axis=dim)
    return block


def sent_to_all(shard, axis):
    peers = lax.axis_size(axis)
    return lax.all_to_all(
        jnp.broadcast_to(shard[None], (peers, *shard.shape)), axis, 0, 0, tiled=True
    )


def taken_together(shard, axis):
    everything = sent_to_all(shard, axis)
    return jnp.sum(everything, axis=0)


def in_one_piece(arrays, axis, split_dim, concat_dim, along):
    columns = [a.reshape(*a.shape[:along], -1) for a in arrays]
    both = jnp.concatenate(columns, axis=along)
    out, at, done = (
        lax.all_to_all(both, axis, split_axis=split_dim, concat_axis=concat_dim, tiled=True),
        0,
        [],
    )
    for a, column in zip(arrays, columns):
        section = out[..., at : at + column.shape[along]]
        done.append(section.reshape(*section.shape[:along], *a.shape[along:]))
        at += column.shape[along]
    return tuple(done)


def in_one_piece_2(arrays, axis, split_dim, concat_dim, along):
    ends, at = ([], 0)
    for a in arrays[:-1]:
        at += a.shape[along]
        ends.append(at)
    both = jnp.concatenate(arrays, axis=along)
    return tuple(
        jnp.split(
            lax.all_to_all(both, axis, split_axis=split_dim, concat_axis=concat_dim, tiled=True),
            ends,
            axis=along,
        )
    )


def together(arrays, axis):
    ravelled, at, done = (jnp.concatenate([a.reshape(-1) for a in arrays]), 0, [])
    subtotal = lax.psum(ravelled, axis)
    for a in arrays:
        done.append(subtotal[at : at + a.size].reshape(a.shape))
        at += a.size
    return tuple(done)


def summed_everywhere(arrays):
    flat = jnp.concatenate([a.reshape(-1) for a in arrays])
    n_cols, n_mem = lax.axis_size("cols"), lax.axis_size("mem")
    size = flat.shape[0]
    width = -(-size // (n_cols * n_mem))
    flat = jnp.pad(flat, (0, width * n_cols * n_mem - size))
    part = lax.all_to_all(flat.reshape(n_mem, n_cols * width), "mem", 0, 0, tiled=True)
    pieces = lax.all_to_all(jnp.sum(part, axis=0).reshape(n_cols, width), "cols", 0, 0, tiled=True)
    mine = jnp.sum(pieces, axis=0)
    back = sent_to_all(mine, "cols").reshape(-1)
    total, at, done = sent_to_all(back, "mem").reshape(-1), 0, []
    for a in arrays:
        done.append(total[at : at + a.size].reshape(a.shape))
        at += a.size
    return tuple(done)


def joined_along(parts, dim):
    parts = jnp.moveaxis(parts, 0, dim)
    lengths = parts.shape
    return parts.reshape(*lengths[:dim], lengths[dim] * lengths[dim + 1], *lengths[dim + 2 :])


def collect(shard, axis, dim):
    return joined_along(sent_to_all(shard, axis), dim)


def _eliminate(a_ref, low_ref, inv_ref, m_ref):
    n = a_ref.shape[0]
    tile = 16
    rows = lax.broadcasted_iota(jnp.int32, (n, n), 0)
    cols = lax.broadcasted_iota(jnp.int32, (n, n), 1)
    sub = lax.broadcasted_iota(jnp.int32, (tile, 1), 0)
    lane = lax.broadcasted_iota(jnp.int32, (1, n), 1)
    m_ref[:, :n] = a_ref[...]
    m_ref[:, n:] = (rows == cols).astype(jnp.float32)

    def step(j, carry):
        row = m_ref[pl.ds(j, 1), :]
        pivot = jnp.sum(jnp.where(lane == j, row[:, :n], 0.0), axis=1, keepdims=True)
        for t in range(n // tile):

            @pl.when(t * tile + tile - 1 > j)
            def _():
                block = m_ref[t * tile : (t + 1) * tile, :]
                column = jnp.sum(jnp.where(lane == j, block[:, :n], 0.0), axis=1, keepdims=True)
                factor = jnp.where(sub + t * tile > j, column / pivot, 0.0)
                m_ref[t * tile : (t + 1) * tile, :] = block - factor * row

        return carry

    lax.fori_loop(0, n, step, 0)
    whole = m_ref[...]
    diag = jnp.sum(jnp.where(rows == cols, whole[:, :n], 0.0), axis=1, keepdims=True)
    scale = 1.0 / jnp.sqrt(diag)
    low_ref[...] = jnp.where(rows <= cols, whole[:, :n] * scale, 0.0)
    inv_ref[...] = whole[:, n:] * scale


def factor_block(block):
    width = block.shape[0]
    symmetric = jnp.tril(block) + jnp.tril(block, -1).T
    square = jax.ShapeDtypeStruct((width, width), jnp.float32)
    upper, inverse = pl.pallas_call(
        _eliminate,
        out_shape=(square, square),
        in_specs=[pl.BlockSpec(memory_space=pltpu.VMEM)],
        out_specs=(pl.BlockSpec(memory_space=pltpu.VMEM), pl.BlockSpec(memory_space=pltpu.VMEM)),
        scratch_shapes=[pltpu.VMEM((width, 2 * width), jnp.float32)],
    )(symmetric)
    return upper.T, inverse


def factor_inverse(gram):
    top = lax.Precision.HIGHEST
    order = gram.shape[0]
    step_size = min(128, order)
    identity = jnp.eye(order, dtype=jnp.float32)
    chol = jnp.zeros((order, order), jnp.float32)
    chol_inverse = jnp.zeros((order, order), jnp.float32)
    for block_index in range(order // step_size):
        begin = block_index * step_size
        finish = begin + step_size
        panel = gram[begin:, begin:finish]
        if block_index > 0:
            panel = panel - jnp.dot(
                chol[begin:, :begin], chol[begin:finish, :begin].T, precision=top
            )
        diag_low, diag_inverse = factor_block(panel[:step_size])
        below = jnp.dot(panel[step_size:], diag_inverse.T, precision=top)
        chol = chol.at[begin:, begin:finish].set(jnp.concatenate([diag_low, below], axis=0))
        right_side = identity[begin:finish]
        if block_index > 0:
            right_side = right_side - jnp.dot(
                chol[begin:finish, :begin], chol_inverse[:begin], precision=top
            )
        chol_inverse = chol_inverse.at[begin:finish].set(
            jnp.dot(diag_inverse, right_side, precision=top)
        )
    return chol_inverse


def body(column_profiles, w_in, w_depth, w_out, obs_op, foot, owner, obs, rinv, inflation):
    top = lax.Precision.HIGHEST
    n_cols = lax.axis_size("cols")
    n_mem = lax.axis_size("mem")
    mem_dev = column_profiles.shape[2]
    members = mem_dev * n_mem
    src_b = foot.shape[0]
    col_dev = column_profiles.shape[0]
    widened = extended(column_profiles, (("cols", 0),), 1)
    hidden = jax.nn.gelu(
        jnp.einsum("kcm,ch->khm", widened, w_in, preferred_element_type=jnp.float32)
    ).astype(jnp.bfloat16)
    mixed = (
        w_depth[0][None, :, None] * hidden[:-2]
        + w_depth[1][None, :, None] * hidden[1:-1]
        + w_depth[2][None, :, None] * hidden[2:]
    ).astype(jnp.bfloat16)
    predicted_column = column_profiles.astype(jnp.float32) + jnp.einsum(
        "khm,hc->kcm", mixed, w_out, preferred_element_type=jnp.float32
    )
    grand_accumulation = taken_together(jnp.sum(predicted_column, axis=2), "mem")
    profile_average = grand_accumulation / members
    departure_from_average = predicted_column - profile_average[:, :, None]
    pobs = jnp.einsum("kcm,co->kom", departure_from_average, obs_op, precision=top)
    mobs = jnp.dot(profile_average, obs_op, precision=top)
    hits = (foot[:, :, None] == jnp.arange(col_dev, dtype=jnp.int32)[None, None, :]).astype(
        jnp.float32
    )
    counts = jnp.sum((foot >= 0).astype(jnp.float32), axis=1)
    onehot = jnp.sum(hits, axis=1) / counts[:, None]
    fpert = jnp.einsum("bk,kom->bom", onehot, pobs, precision=top)
    fmean = jnp.dot(onehot, mobs, precision=top)
    scale = 1.0 / math.sqrt(members - 1)
    spread = (rinv[:, :, None] * fpert * scale).astype(jnp.bfloat16)
    innov = (rinv * (obs - fmean)).astype(jnp.bfloat16)
    every_inflation = sent_to_all(inflation, "cols").reshape(-1)
    factor = every_inflation[owner[:, 0]] ** 2
    quarter = src_b // n_mem
    first_batch = lax.axis_index("mem") * quarter
    pertb = departure_from_average.astype(jnp.bfloat16)
    own = pertb.shape[0] * pertb.shape[1]
    outgoing = jnp.concatenate(
        [
            jnp.broadcast_to(pertb.reshape(1, own, mem_dev), (n_mem, own, mem_dev)),
            spread.reshape(n_mem, -1, mem_dev),
        ],
        axis=1,
    )
    incoming = lax.all_to_all(outgoing, "mem", 0, 0, tiled=True)
    every_pertb = joined_along(incoming[:, :own].reshape(n_mem, *pertb.shape), 2)
    portion = joined_along(
        incoming[:, own:].reshape(n_mem, quarter, *spread.shape[1:]), 2
    ).astype(jnp.float32)
    innov_part = lax.dynamic_slice_in_dim(innov, first_batch, quarter, 0)
    factor_part = lax.dynamic_slice_in_dim(factor, first_batch, quarter, 0)
    weighted = portion * factor_part[:, None, None]
    whole = jnp.einsum("qom,qoj->mj", weighted, portion, precision=top)
    vector = jnp.einsum("qom,qo->m", weighted, innov_part.astype(jnp.float32), precision=top)
    half = members // 2
    folded = jnp.tril(whole[half:, half:]) + jnp.tril(whole[:half, :half], -1).T
    lower_left, folded, diagonal, vec_all = summed_everywhere(
        (whole[half:, :half], folded, jnp.diagonal(whole[:half, :half]), vector)
    )
    upper_left = jnp.triu(folded, 1).T + jnp.diag(diagonal)
    gram_low = jnp.concatenate(
        [
            jnp.concatenate([upper_left, jnp.zeros_like(upper_left)], axis=1),
            jnp.concatenate([lower_left, jnp.tril(folded)], axis=1),
        ],
        axis=0,
    )
    gram = jnp.eye(members, dtype=jnp.float32) + gram_low
    chol_inverse = factor_inverse(gram)
    weights = jnp.dot(chol_inverse.T, jnp.dot(chol_inverse, vec_all, precision=top), precision=top)
    first = lax.axis_index("mem") * mem_dev
    tinv_mine = lax.dynamic_slice_in_dim(chol_inverse, first, mem_dev, 0).T
    mix_w = (weights[:, None] * scale + tinv_mine).astype(jnp.bfloat16)
    moved = jnp.einsum("kcm,mj->kcj", every_pertb, mix_w, preferred_element_type=jnp.float32)
    return (profile_average[:, :, None] + moved).astype(jnp.bfloat16)


def solution(mesh):
    placed = (
        P("cols", None, "mem"),
        P(),
        P(),
        P(),
        P(),
        P("cols", None),
        P("cols", None),
        P("cols", None),
        P("cols", None),
        P("cols"),
    )
    return jax.shard_map(
        body, mesh=mesh, in_specs=placed, out_specs=P("cols", None, "mem"), check_vma=False
    )
```

```python
import math

import jax
import jax.numpy as jnp
from jax import lax
from jax.experimental import pallas as pl
from jax.experimental.pallas import tpu as pltpu
from jax.sharding import PartitionSpec as P


def extended(block, sides, width):
    for axis, dim in sides:
        count = lax.axis_size(axis)
        forward = [(i, i + 1) for i in range(count - 1)]
        backward = [(target, source) for source, target in forward]
        low = lax.ppermute(
            lax.slice_in_dim(block, block.shape[dim] - width, None, axis=dim), axis, forward
        )
        high = lax.ppermute(lax.slice_in_dim(block, 0, width, axis=dim), axis, backward)
        block = jnp.concatenate([low, block, high], axis=dim)
    return block


def sent_to_all(shard, axis):
    peers = lax.axis_size(axis)
    return lax.all_to_all(
        jnp.broadcast_to(shard[None], (peers, *shard.shape)), axis, 0, 0, tiled=True
    )


def taken_together(shard, axis):
    everything = sent_to_all(shard, axis)
    return jnp.sum(everything, axis=0)


def in_one_piece(arrays, axis, split_dim, concat_dim, along):
    columns = [a.reshape(*a.shape[:along], -1) for a in arrays]
    both = jnp.concatenate(columns, axis=along)
    out, at, done = (
        lax.all_to_all(both, axis, split_axis=split_dim, concat_axis=concat_dim, tiled=True),
        0,
        [],
    )
    for a, column in zip(arrays, columns):
        section = out[..., at : at + column.shape[along]]
        done.append(section.reshape(*section.shape[:along], *a.shape[along:]))
        at += column.shape[along]
    return tuple(done)


def in_one_piece_2(arrays, axis, split_dim, concat_dim, along):
    ends, at = ([], 0)
    for a in arrays[:-1]:
        at += a.shape[along]
        ends.append(at)
    both = jnp.concatenate(arrays, axis=along)
    return tuple(
        jnp.split(
            lax.all_to_all(both, axis, split_axis=split_dim, concat_axis=concat_dim, tiled=True),
            ends,
            axis=along,
        )
    )


def together(arrays, axis):
    ravelled, at, done = (jnp.concatenate([a.reshape(-1) for a in arrays]), 0, [])
    subtotal = lax.psum(ravelled, axis)
    for a in arrays:
        done.append(subtotal[at : at + a.size].reshape(a.shape))
        at += a.size
    return tuple(done)


def summed_everywhere(arrays):
    flat = jnp.concatenate([a.reshape(-1) for a in arrays])
    n_cols, n_mem = lax.axis_size("cols"), lax.axis_size("mem")
    size = flat.shape[0]
    width = -(-size // (n_cols * n_mem))
    flat = jnp.pad(flat, (0, width * n_cols * n_mem - size))
    part = lax.all_to_all(flat.reshape(n_mem, n_cols * width), "mem", 0, 0, tiled=True)
    pieces = lax.all_to_all(jnp.sum(part, axis=0).reshape(n_cols, width), "cols", 0, 0, tiled=True)
    mine = jnp.sum(pieces, axis=0)
    back = sent_to_all(mine, "cols").reshape(-1)
    total, at, done = sent_to_all(back, "mem").reshape(-1), 0, []
    for a in arrays:
        done.append(total[at : at + a.size].reshape(a.shape))
        at += a.size
    return tuple(done)


def joined_along(parts, dim):
    parts = jnp.moveaxis(parts, 0, dim)
    lengths = parts.shape
    return parts.reshape(*lengths[:dim], lengths[dim] * lengths[dim + 1], *lengths[dim + 2 :])


def collect(shard, axis, dim):
    return joined_along(sent_to_all(shard, axis), dim)


def _eliminate(a_ref, low_ref, inv_ref, m_ref):
    n = a_ref.shape[0]
    sub = lax.broadcasted_iota(jnp.int32, (n, 1), 0)
    lane = lax.broadcasted_iota(jnp.int32, (1, n), 1)
    rows = lax.broadcasted_iota(jnp.int32, (n, n), 0)
    cols = lax.broadcasted_iota(jnp.int32, (n, n), 1)
    m_ref[:, :n] = a_ref[...]
    m_ref[:, n:] = (rows == cols).astype(jnp.float32)

    def step(j, carry):
        row = m_ref[pl.ds(j, 1), :]
        whole = m_ref[...]
        column = jnp.sum(jnp.where(lane == j, whole[:, :n], 0.0), axis=1, keepdims=True)
        pivot = jnp.sum(jnp.where(lane == j, row[:, :n], 0.0), axis=1, keepdims=True)
        factor = jnp.where(sub > j, column * (1.0 / pivot), 0.0)
        m_ref[...] = whole - factor * row
        return carry

    lax.fori_loop(0, n, step, 0, unroll=2)
    whole = m_ref[...]
    diag = jnp.sum(jnp.where(rows == cols, whole[:, :n], 0.0), axis=1, keepdims=True)
    scale = 1.0 / jnp.sqrt(diag)
    low_ref[...] = jnp.where(rows <= cols, whole[:, :n] * scale, 0.0)
    inv_ref[...] = whole[:, n:] * scale


def factor_block(block):
    width = block.shape[0]
    symmetric = jnp.tril(block) + jnp.tril(block, -1).T
    square = jax.ShapeDtypeStruct((width, width), jnp.float32)
    upper, inverse = pl.pallas_call(
        _eliminate,
        out_shape=(square, square),
        in_specs=[pl.BlockSpec(memory_space=pltpu.VMEM)],
        out_specs=(pl.BlockSpec(memory_space=pltpu.VMEM), pl.BlockSpec(memory_space=pltpu.VMEM)),
        scratch_shapes=[pltpu.VMEM((width, 2 * width), jnp.float32)],
    )(symmetric)
    return upper.T, inverse


def factor_inverse(gram):
    top = lax.Precision.HIGHEST
    order = gram.shape[0]
    step_size = min(128, order)
    identity = jnp.eye(order, dtype=jnp.float32)
    chol = jnp.zeros((order, order), jnp.float32)
    chol_inverse = jnp.zeros((order, order), jnp.float32)
    for block_index in range(order // step_size):
        begin = block_index * step_size
        finish = begin + step_size
        panel = gram[begin:, begin:finish]
        if block_index > 0:
            panel = panel - jnp.dot(
                chol[begin:, :begin], chol[begin:finish, :begin].T, precision=top
            )
        diag_low, diag_inverse = factor_block(panel[:step_size])
        below = jnp.dot(panel[step_size:], diag_inverse.T, precision=top)
        chol = chol.at[begin:, begin:finish].set(jnp.concatenate([diag_low, below], axis=0))
        right_side = identity[begin:finish]
        if block_index > 0:
            right_side = right_side - jnp.dot(
                chol[begin:finish, :begin], chol_inverse[:begin], precision=top
            )
        chol_inverse = chol_inverse.at[begin:finish].set(
            jnp.dot(diag_inverse, right_side, precision=top)
        )
    return chol_inverse


def body(column_profiles, w_in, w_depth, w_out, obs_op, foot, owner, obs, rinv, inflation):
    top = lax.Precision.HIGHEST
    n_cols = lax.axis_size("cols")
    n_mem = lax.axis_size("mem")
    mem_dev = column_profiles.shape[2]
    members = mem_dev * n_mem
    src_b = foot.shape[0]
    col_dev = column_profiles.shape[0]
    widened = extended(column_profiles, (("cols", 0),), 1)
    hidden = jax.nn.gelu(
        jnp.einsum("kcm,ch->khm", widened, w_in, preferred_element_type=jnp.float32)
    ).astype(jnp.bfloat16)
    mixed = (
        w_depth[0][None, :, None] * hidden[:-2]
        + w_depth[1][None, :, None] * hidden[1:-1]
        + w_depth[2][None, :, None] * hidden[2:]
    ).astype(jnp.bfloat16)
    predicted_column = column_profiles.astype(jnp.float32) + jnp.einsum(
        "khm,hc->kcm", mixed, w_out, preferred_element_type=jnp.float32
    )
    grand_accumulation = taken_together(jnp.sum(predicted_column, axis=2), "mem")
    profile_average = grand_accumulation / members
    departure_from_average = predicted_column - profile_average[:, :, None]
    pobs = jnp.einsum("kcm,co->kom", departure_from_average, obs_op, precision=top)
    mobs = jnp.dot(profile_average, obs_op, precision=top)
    hits = (foot[:, :, None] == jnp.arange(col_dev, dtype=jnp.int32)[None, None, :]).astype(
        jnp.float32
    )
    counts = jnp.sum((foot >= 0).astype(jnp.float32), axis=1)
    onehot = jnp.sum(hits, axis=1) / counts[:, None]
    fpert = jnp.einsum("bk,kom->bom", onehot, pobs, precision=top)
    fmean = jnp.dot(onehot, mobs, precision=top)
    scale = 1.0 / math.sqrt(members - 1)
    spread = (rinv[:, :, None] * fpert * scale).astype(jnp.bfloat16)
    innov = (rinv * (obs - fmean)).astype(jnp.bfloat16)
    every_inflation = sent_to_all(inflation, "cols").reshape(-1)
    factor = every_inflation[owner[:, 0]] ** 2
    quarter = src_b // n_mem
    first_batch = lax.axis_index("mem") * quarter
    pertb = departure_from_average.astype(jnp.bfloat16)
    own = pertb.shape[0] * pertb.shape[1]
    outgoing = jnp.concatenate(
        [
            jnp.broadcast_to(pertb.reshape(1, own, mem_dev), (n_mem, own, mem_dev)),
            spread.reshape(n_mem, -1, mem_dev),
        ],
        axis=1,
    )
    incoming = lax.all_to_all(outgoing, "mem", 0, 0, tiled=True)
    every_pertb = joined_along(incoming[:, :own].reshape(n_mem, *pertb.shape), 2)
    portion = joined_along(
        incoming[:, own:].reshape(n_mem, quarter, *spread.shape[1:]), 2
    ).astype(jnp.float32)
    innov_part = lax.dynamic_slice_in_dim(innov, first_batch, quarter, 0)
    factor_part = lax.dynamic_slice_in_dim(factor, first_batch, quarter, 0)
    weighted = portion * factor_part[:, None, None]
    whole = jnp.einsum("qom,qoj->mj", weighted, portion, precision=top)
    vector = jnp.einsum("qom,qo->m", weighted, innov_part.astype(jnp.float32), precision=top)
    half = members // 2
    folded = jnp.tril(whole[half:, half:]) + jnp.tril(whole[:half, :half], -1).T
    lower_left, folded, diagonal, vec_all = summed_everywhere(
        (whole[half:, :half], folded, jnp.diagonal(whole[:half, :half]), vector)
    )
    upper_left = jnp.triu(folded, 1).T + jnp.diag(diagonal)
    gram_low = jnp.concatenate(
        [
            jnp.concatenate([upper_left, jnp.zeros_like(upper_left)], axis=1),
            jnp.concatenate([lower_left, jnp.tril(folded)], axis=1),
        ],
        axis=0,
    )
    gram = jnp.eye(members, dtype=jnp.float32) + gram_low
    chol_inverse = factor_inverse(gram)
    weights = jnp.dot(chol_inverse.T, jnp.dot(chol_inverse, vec_all, precision=top), precision=top)
    first = lax.axis_index("mem") * mem_dev
    tinv_mine = lax.dynamic_slice_in_dim(chol_inverse, first, mem_dev, 0).T
    mix_w = (weights[:, None] * scale + tinv_mine).astype(jnp.bfloat16)
    moved = jnp.einsum("kcm,mj->kcj", every_pertb, mix_w, preferred_element_type=jnp.float32)
    return (profile_average[:, :, None] + moved).astype(jnp.bfloat16)


def solution(mesh):
    placed = (
        P("cols", None, "mem"),
        P(),
        P(),
        P(),
        P(),
        P("cols", None),
        P("cols", None),
        P("cols", None),
        P("cols", None),
        P("cols"),
    )
    return jax.shard_map(
        body, mesh=mesh, in_specs=placed, out_specs=P("cols", None, "mem"), check_vma=False
    )
```

```python
import math

import jax
import jax.numpy as jnp
from jax import lax
from jax.experimental import pallas as pl
from jax.experimental.pallas import tpu as pltpu
from jax.sharding import PartitionSpec as P


def extended(block, sides, width):
    for axis, dim in sides:
        count = lax.axis_size(axis)
        forward = [(i, i + 1) for i in range(count - 1)]
        backward = [(target, source) for source, target in forward]
        low = lax.ppermute(
            lax.slice_in_dim(block, block.shape[dim] - width, None, axis=dim), axis, forward
        )
        high = lax.ppermute(lax.slice_in_dim(block, 0, width, axis=dim), axis, backward)
        block = jnp.concatenate([low, block, high], axis=dim)
    return block


def sent_to_all(shard, axis):
    peers = lax.axis_size(axis)
    return lax.all_to_all(
        jnp.broadcast_to(shard[None], (peers, *shard.shape)), axis, 0, 0, tiled=True
    )


def taken_together(shard, axis):
    everything = sent_to_all(shard, axis)
    return jnp.sum(everything, axis=0)


def in_one_piece(arrays, axis, split_dim, concat_dim, along):
    columns = [a.reshape(*a.shape[:along], -1) for a in arrays]
    both = jnp.concatenate(columns, axis=along)
    out, at, done = (
        lax.all_to_all(both, axis, split_axis=split_dim, concat_axis=concat_dim, tiled=True),
        0,
        [],
    )
    for a, column in zip(arrays, columns):
        section = out[..., at : at + column.shape[along]]
        done.append(section.reshape(*section.shape[:along], *a.shape[along:]))
        at += column.shape[along]
    return tuple(done)


def in_one_piece_2(arrays, axis, split_dim, concat_dim, along):
    ends, at = ([], 0)
    for a in arrays[:-1]:
        at += a.shape[along]
        ends.append(at)
    both = jnp.concatenate(arrays, axis=along)
    return tuple(
        jnp.split(
            lax.all_to_all(both, axis, split_axis=split_dim, concat_axis=concat_dim, tiled=True),
            ends,
            axis=along,
        )
    )


def together(arrays, axis):
    ravelled, at, done = (jnp.concatenate([a.reshape(-1) for a in arrays]), 0, [])
    subtotal = lax.psum(ravelled, axis)
    for a in arrays:
        done.append(subtotal[at : at + a.size].reshape(a.shape))
        at += a.size
    return tuple(done)


def summed_everywhere(arrays):
    flat = jnp.concatenate([a.reshape(-1) for a in arrays])
    n_cols, n_mem = lax.axis_size("cols"), lax.axis_size("mem")
    size = flat.shape[0]
    width = -(-size // (n_cols * n_mem))
    flat = jnp.pad(flat, (0, width * n_cols * n_mem - size))
    part = lax.all_to_all(flat.reshape(n_mem, n_cols * width), "mem", 0, 0, tiled=True)
    pieces = lax.all_to_all(jnp.sum(part, axis=0).reshape(n_cols, width), "cols", 0, 0, tiled=True)
    mine = jnp.sum(pieces, axis=0)
    back = sent_to_all(mine, "cols").reshape(-1)
    total, at, done = sent_to_all(back, "mem").reshape(-1), 0, []
    for a in arrays:
        done.append(total[at : at + a.size].reshape(a.shape))
        at += a.size
    return tuple(done)


def joined_along(parts, dim):
    parts = jnp.moveaxis(parts, 0, dim)
    lengths = parts.shape
    return parts.reshape(*lengths[:dim], lengths[dim] * lengths[dim + 1], *lengths[dim + 2 :])


def collect(shard, axis, dim):
    return joined_along(sent_to_all(shard, axis), dim)


def _eliminate(a_ref, low_ref, inv_ref, m_ref):
    n = a_ref.shape[0]
    sub = lax.broadcasted_iota(jnp.int32, (n, 1), 0)
    lane = lax.broadcasted_iota(jnp.int32, (1, n), 1)
    rows = lax.broadcasted_iota(jnp.int32, (n, n), 0)
    cols = lax.broadcasted_iota(jnp.int32, (n, n), 1)
    given = a_ref[...]
    m_ref[:, :n] = jnp.where(rows >= cols, given, given.T)
    m_ref[:, n:] = (rows == cols).astype(jnp.float32)

    def step(j, carry):
        row = m_ref[pl.ds(j, 1), :]
        whole = m_ref[...]
        column = jnp.sum(jnp.where(lane == j, whole[:, :n], 0.0), axis=1, keepdims=True)
        pivot = jnp.sum(jnp.where(lane == j, row[:, :n], 0.0), axis=1, keepdims=True)
        factor = jnp.where(sub > j, column * (1.0 / pivot), 0.0)
        m_ref[...] = whole - factor * row
        return carry

    lax.fori_loop(0, n, step, 0, unroll=2)
    whole = m_ref[...]
    diag = jnp.sum(jnp.where(rows == cols, whole[:, :n], 0.0), axis=1, keepdims=True)
    scale = 1.0 / jnp.sqrt(diag)
    low_ref[...] = jnp.where(rows <= cols, whole[:, :n] * scale, 0.0).T
    inv_ref[...] = whole[:, n:] * scale


def factor_block(block):
    width = block.shape[0]
    square = jax.ShapeDtypeStruct((width, width), jnp.float32)
    lower, inverse = pl.pallas_call(
        _eliminate,
        out_shape=(square, square),
        in_specs=[pl.BlockSpec(memory_space=pltpu.VMEM)],
        out_specs=(pl.BlockSpec(memory_space=pltpu.VMEM), pl.BlockSpec(memory_space=pltpu.VMEM)),
        scratch_shapes=[pltpu.VMEM((width, 2 * width), jnp.float32)],
    )(block)
    return lower, inverse


def factor_inverse(gram):
    top = lax.Precision.HIGHEST
    order = gram.shape[0]
    step_size = min(128, order)
    identity = jnp.eye(order, dtype=jnp.float32)
    chol = jnp.zeros((order, order), jnp.float32)
    chol_inverse = jnp.zeros((order, order), jnp.float32)
    for block_index in range(order // step_size):
        begin = block_index * step_size
        finish = begin + step_size
        panel = gram[begin:, begin:finish]
        if block_index > 0:
            panel = panel - jnp.dot(
                chol[begin:, :begin], chol[begin:finish, :begin].T, precision=top
            )
        diag_low, diag_inverse = factor_block(panel[:step_size])
        below = jnp.dot(panel[step_size:], diag_inverse.T, precision=top)
        chol = chol.at[begin:, begin:finish].set(jnp.concatenate([diag_low, below], axis=0))
        right_side = identity[begin:finish]
        if block_index > 0:
            right_side = right_side - jnp.dot(
                chol[begin:finish, :begin], chol_inverse[:begin], precision=top
            )
        chol_inverse = chol_inverse.at[begin:finish].set(
            jnp.dot(diag_inverse, right_side, precision=top)
        )
    return chol_inverse


def body(column_profiles, w_in, w_depth, w_out, obs_op, foot, owner, obs, rinv, inflation):
    top = lax.Precision.HIGHEST
    n_cols = lax.axis_size("cols")
    n_mem = lax.axis_size("mem")
    mem_dev = column_profiles.shape[2]
    members = mem_dev * n_mem
    src_b = foot.shape[0]
    col_dev = column_profiles.shape[0]
    widened = extended(column_profiles, (("cols", 0),), 1)
    hidden = jax.nn.gelu(
        jnp.einsum("kcm,ch->khm", widened, w_in, preferred_element_type=jnp.float32)
    ).astype(jnp.bfloat16)
    mixed = (
        w_depth[0][None, :, None] * hidden[:-2]
        + w_depth[1][None, :, None] * hidden[1:-1]
        + w_depth[2][None, :, None] * hidden[2:]
    ).astype(jnp.bfloat16)
    predicted_column = column_profiles.astype(jnp.float32) + jnp.einsum(
        "khm,hc->kcm", mixed, w_out, preferred_element_type=jnp.float32
    )
    grand_accumulation = taken_together(jnp.sum(predicted_column, axis=2), "mem")
    profile_average = grand_accumulation / members
    departure_from_average = predicted_column - profile_average[:, :, None]
    pobs = jnp.einsum("kcm,co->kom", departure_from_average, obs_op, precision=top)
    mobs = jnp.dot(profile_average, obs_op, precision=top)
    hits = (foot[:, :, None] == jnp.arange(col_dev, dtype=jnp.int32)[None, None, :]).astype(
        jnp.float32
    )
    counts = jnp.sum((foot >= 0).astype(jnp.float32), axis=1)
    onehot = jnp.sum(hits, axis=1) / counts[:, None]
    fpert = jnp.einsum("bk,kom->bom", onehot, pobs, precision=top)
    fmean = jnp.dot(onehot, mobs, precision=top)
    scale = 1.0 / math.sqrt(members - 1)
    spread = (rinv[:, :, None] * fpert * scale).astype(jnp.bfloat16)
    innov = (rinv * (obs - fmean)).astype(jnp.bfloat16)
    every_inflation = sent_to_all(inflation, "cols").reshape(-1)
    factor = every_inflation[owner[:, 0]] ** 2
    quarter = src_b // n_mem
    first_batch = lax.axis_index("mem") * quarter
    pertb = departure_from_average.astype(jnp.bfloat16)
    own = pertb.shape[0] * pertb.shape[1]
    outgoing = jnp.concatenate(
        [
            jnp.broadcast_to(pertb.reshape(1, own, mem_dev), (n_mem, own, mem_dev)),
            spread.reshape(n_mem, -1, mem_dev),
        ],
        axis=1,
    )
    incoming = lax.all_to_all(outgoing, "mem", 0, 0, tiled=True)
    every_pertb = joined_along(incoming[:, :own].reshape(n_mem, *pertb.shape), 2)
    portion = joined_along(
        incoming[:, own:].reshape(n_mem, quarter, *spread.shape[1:]), 2
    ).astype(jnp.float32)
    innov_part = lax.dynamic_slice_in_dim(innov, first_batch, quarter, 0)
    factor_part = lax.dynamic_slice_in_dim(factor, first_batch, quarter, 0)
    weighted = portion * factor_part[:, None, None]
    whole = jnp.einsum("qom,qoj->mj", weighted, portion, precision=top)
    vector = jnp.einsum("qom,qo->m", weighted, innov_part.astype(jnp.float32), precision=top)
    half = members // 2
    folded = jnp.tril(whole[half:, half:]) + jnp.tril(whole[:half, :half], -1).T
    lower_left, folded, diagonal, vec_all = summed_everywhere(
        (whole[half:, :half], folded, jnp.diagonal(whole[:half, :half]), vector)
    )
    upper_left = jnp.triu(folded, 1).T + jnp.diag(diagonal)
    gram_low = jnp.concatenate(
        [
            jnp.concatenate([upper_left, jnp.zeros_like(upper_left)], axis=1),
            jnp.concatenate([lower_left, jnp.tril(folded)], axis=1),
        ],
        axis=0,
    )
    gram = jnp.eye(members, dtype=jnp.float32) + gram_low
    chol_inverse = factor_inverse(gram)
    weights = jnp.dot(chol_inverse.T, jnp.dot(chol_inverse, vec_all, precision=top), precision=top)
    first = lax.axis_index("mem") * mem_dev
    tinv_mine = lax.dynamic_slice_in_dim(chol_inverse, first, mem_dev, 0).T
    mix_w = (weights[:, None] * scale + tinv_mine).astype(jnp.bfloat16)
    moved = jnp.einsum("kcm,mj->kcj", every_pertb, mix_w, preferred_element_type=jnp.float32)
    return (profile_average[:, :, None] + moved).astype(jnp.bfloat16)


def solution(mesh):
    placed = (
        P("cols", None, "mem"),
        P(),
        P(),
        P(),
        P(),
        P("cols", None),
        P("cols", None),
        P("cols", None),
        P("cols", None),
        P("cols"),
    )
    return jax.shard_map(
        body, mesh=mesh, in_specs=placed, out_specs=P("cols", None, "mem"), check_vma=False
    )
```

```python
import math

import jax
import jax.numpy as jnp
from jax import lax
from jax.experimental import pallas as pl
from jax.experimental.pallas import tpu as pltpu
from jax.sharding import PartitionSpec as P


def extended(block, sides, width):
    for axis, dim in sides:
        count = lax.axis_size(axis)
        forward = [(i, i + 1) for i in range(count - 1)]
        backward = [(target, source) for source, target in forward]
        low = lax.ppermute(
            lax.slice_in_dim(block, block.shape[dim] - width, None, axis=dim), axis, forward
        )
        high = lax.ppermute(lax.slice_in_dim(block, 0, width, axis=dim), axis, backward)
        block = jnp.concatenate([low, block, high], axis=dim)
    return block


def sent_to_all(shard, axis):
    peers = lax.axis_size(axis)
    return lax.all_to_all(
        jnp.broadcast_to(shard[None], (peers, *shard.shape)), axis, 0, 0, tiled=True
    )


def taken_together(shard, axis):
    everything = sent_to_all(shard, axis)
    return jnp.sum(everything, axis=0)


def in_one_piece(arrays, axis, split_dim, concat_dim, along):
    columns = [a.reshape(*a.shape[:along], -1) for a in arrays]
    both = jnp.concatenate(columns, axis=along)
    out, at, done = (
        lax.all_to_all(both, axis, split_axis=split_dim, concat_axis=concat_dim, tiled=True),
        0,
        [],
    )
    for a, column in zip(arrays, columns):
        section = out[..., at : at + column.shape[along]]
        done.append(section.reshape(*section.shape[:along], *a.shape[along:]))
        at += column.shape[along]
    return tuple(done)


def in_one_piece_2(arrays, axis, split_dim, concat_dim, along):
    ends, at = ([], 0)
    for a in arrays[:-1]:
        at += a.shape[along]
        ends.append(at)
    both = jnp.concatenate(arrays, axis=along)
    return tuple(
        jnp.split(
            lax.all_to_all(both, axis, split_axis=split_dim, concat_axis=concat_dim, tiled=True),
            ends,
            axis=along,
        )
    )


def together(arrays, axis):
    ravelled, at, done = (jnp.concatenate([a.reshape(-1) for a in arrays]), 0, [])
    subtotal = lax.psum(ravelled, axis)
    for a in arrays:
        done.append(subtotal[at : at + a.size].reshape(a.shape))
        at += a.size
    return tuple(done)


def summed_everywhere(arrays):
    flat = jnp.concatenate([a.reshape(-1) for a in arrays])
    n_cols, n_mem = lax.axis_size("cols"), lax.axis_size("mem")
    size = flat.shape[0]
    width = -(-size // (n_cols * n_mem))
    flat = jnp.pad(flat, (0, width * n_cols * n_mem - size))
    part = lax.all_to_all(flat.reshape(n_mem, n_cols * width), "mem", 0, 0, tiled=True)
    pieces = lax.all_to_all(jnp.sum(part, axis=0).reshape(n_cols, width), "cols", 0, 0, tiled=True)
    mine = jnp.sum(pieces, axis=0)
    back = sent_to_all(mine, "cols").reshape(-1)
    total, at, done = sent_to_all(back, "mem").reshape(-1), 0, []
    for a in arrays:
        done.append(total[at : at + a.size].reshape(a.shape))
        at += a.size
    return tuple(done)


def joined_along(parts, dim):
    parts = jnp.moveaxis(parts, 0, dim)
    lengths = parts.shape
    return parts.reshape(*lengths[:dim], lengths[dim] * lengths[dim + 1], *lengths[dim + 2 :])


def collect(shard, axis, dim):
    return joined_along(sent_to_all(shard, axis), dim)


def _eliminate(a_ref, low_ref, inv_ref, left_ref, right_ref):
    n = a_ref.shape[0]
    sub = lax.broadcasted_iota(jnp.int32, (n, 1), 0)
    lane = lax.broadcasted_iota(jnp.int32, (1, n), 1)
    rows = lax.broadcasted_iota(jnp.int32, (n, n), 0)
    cols = lax.broadcasted_iota(jnp.int32, (n, n), 1)
    given = a_ref[...]
    left_ref[...] = jnp.where(rows >= cols, given, given.T)
    right_ref[...] = (rows == cols).astype(jnp.float32)

    def step(j, carry):
        row = left_ref[pl.ds(j, 1), :]
        other = right_ref[pl.ds(j, 1), :]
        whole = left_ref[...]
        column = jnp.sum(jnp.where(lane == j, whole, 0.0), axis=1, keepdims=True)
        pivot = jnp.sum(jnp.where(lane == j, row, 0.0), axis=1, keepdims=True)
        factor = jnp.where(sub > j, column * (1.0 / pivot), 0.0)
        left_ref[...] = whole - factor * row
        right_ref[...] = right_ref[...] - factor * other
        return carry

    lax.fori_loop(0, n, step, 0, unroll=2)
    whole = left_ref[...]
    diag = jnp.sum(jnp.where(rows == cols, whole, 0.0), axis=1, keepdims=True)
    scale = 1.0 / jnp.sqrt(diag)
    low_ref[...] = jnp.where(rows <= cols, whole * scale, 0.0).T
    inv_ref[...] = right_ref[...] * scale


def factor_block(block):
    width = block.shape[0]
    square = jax.ShapeDtypeStruct((width, width), jnp.float32)
    lower, inverse = pl.pallas_call(
        _eliminate,
        out_shape=(square, square),
        in_specs=[pl.BlockSpec(memory_space=pltpu.VMEM)],
        out_specs=(pl.BlockSpec(memory_space=pltpu.VMEM), pl.BlockSpec(memory_space=pltpu.VMEM)),
        scratch_shapes=[pltpu.VMEM((width, width), jnp.float32)] * 2,
    )(block)
    return lower, inverse


def factor_inverse(gram):
    top = lax.Precision.HIGHEST
    order = gram.shape[0]
    step_size = min(128, order)
    identity = jnp.eye(order, dtype=jnp.float32)
    chol = jnp.zeros((order, order), jnp.float32)
    chol_inverse = jnp.zeros((order, order), jnp.float32)
    for block_index in range(order // step_size):
        begin = block_index * step_size
        finish = begin + step_size
        panel = gram[begin:, begin:finish]
        if block_index > 0:
            panel = panel - jnp.dot(
                chol[begin:, :begin], chol[begin:finish, :begin].T, precision=top
            )
        diag_low, diag_inverse = factor_block(panel[:step_size])
        below = jnp.dot(panel[step_size:], diag_inverse.T, precision=top)
        chol = chol.at[begin:, begin:finish].set(jnp.concatenate([diag_low, below], axis=0))
        right_side = identity[begin:finish]
        if block_index > 0:
            right_side = right_side - jnp.dot(
                chol[begin:finish, :begin], chol_inverse[:begin], precision=top
            )
        chol_inverse = chol_inverse.at[begin:finish].set(
            jnp.dot(diag_inverse, right_side, precision=top)
        )
    return chol_inverse


def body(column_profiles, w_in, w_depth, w_out, obs_op, foot, owner, obs, rinv, inflation):
    top = lax.Precision.HIGHEST
    n_cols = lax.axis_size("cols")
    n_mem = lax.axis_size("mem")
    mem_dev = column_profiles.shape[2]
    members = mem_dev * n_mem
    src_b = foot.shape[0]
    col_dev = column_profiles.shape[0]
    widened = extended(column_profiles, (("cols", 0),), 1)
    hidden = jax.nn.gelu(
        jnp.einsum("kcm,ch->khm", widened, w_in, preferred_element_type=jnp.float32)
    ).astype(jnp.bfloat16)
    mixed = (
        w_depth[0][None, :, None] * hidden[:-2]
        + w_depth[1][None, :, None] * hidden[1:-1]
        + w_depth[2][None, :, None] * hidden[2:]
    ).astype(jnp.bfloat16)
    predicted_column = column_profiles.astype(jnp.float32) + jnp.einsum(
        "khm,hc->kcm", mixed, w_out, preferred_element_type=jnp.float32
    )
    grand_accumulation = taken_together(jnp.sum(predicted_column, axis=2), "mem")
    profile_average = grand_accumulation / members
    departure_from_average = predicted_column - profile_average[:, :, None]
    pobs = jnp.einsum("kcm,co->kom", departure_from_average, obs_op, precision=top)
    mobs = jnp.dot(profile_average, obs_op, precision=top)
    hits = (foot[:, :, None] == jnp.arange(col_dev, dtype=jnp.int32)[None, None, :]).astype(
        jnp.float32
    )
    counts = jnp.sum((foot >= 0).astype(jnp.float32), axis=1)
    onehot = jnp.sum(hits, axis=1) / counts[:, None]
    fpert = jnp.einsum("bk,kom->bom", onehot, pobs, precision=top)
    fmean = jnp.dot(onehot, mobs, precision=top)
    scale = 1.0 / math.sqrt(members - 1)
    spread = (rinv[:, :, None] * fpert * scale).astype(jnp.bfloat16)
    innov = (rinv * (obs - fmean)).astype(jnp.bfloat16)
    every_inflation = sent_to_all(inflation, "cols").reshape(-1)
    factor = every_inflation[owner[:, 0]] ** 2
    quarter = src_b // n_mem
    first_batch = lax.axis_index("mem") * quarter
    pertb = departure_from_average.astype(jnp.bfloat16)
    own = pertb.shape[0] * pertb.shape[1]
    outgoing = jnp.concatenate(
        [
            jnp.broadcast_to(pertb.reshape(1, own, mem_dev), (n_mem, own, mem_dev)),
            spread.reshape(n_mem, -1, mem_dev),
        ],
        axis=1,
    )
    incoming = lax.all_to_all(outgoing, "mem", 0, 0, tiled=True)
    every_pertb = joined_along(incoming[:, :own].reshape(n_mem, *pertb.shape), 2)
    portion = joined_along(
        incoming[:, own:].reshape(n_mem, quarter, *spread.shape[1:]), 2
    ).astype(jnp.float32)
    innov_part = lax.dynamic_slice_in_dim(innov, first_batch, quarter, 0)
    factor_part = lax.dynamic_slice_in_dim(factor, first_batch, quarter, 0)
    weighted = portion * factor_part[:, None, None]
    whole = jnp.einsum("qom,qoj->mj", weighted, portion, precision=top)
    vector = jnp.einsum("qom,qo->m", weighted, innov_part.astype(jnp.float32), precision=top)
    half = members // 2
    folded = jnp.tril(whole[half:, half:]) + jnp.tril(whole[:half, :half], -1).T
    lower_left, folded, diagonal, vec_all = summed_everywhere(
        (whole[half:, :half], folded, jnp.diagonal(whole[:half, :half]), vector)
    )
    upper_left = jnp.triu(folded, 1).T + jnp.diag(diagonal)
    gram_low = jnp.concatenate(
        [
            jnp.concatenate([upper_left, jnp.zeros_like(upper_left)], axis=1),
            jnp.concatenate([lower_left, jnp.tril(folded)], axis=1),
        ],
        axis=0,
    )
    gram = jnp.eye(members, dtype=jnp.float32) + gram_low
    chol_inverse = factor_inverse(gram)
    weights = jnp.dot(chol_inverse.T, jnp.dot(chol_inverse, vec_all, precision=top), precision=top)
    first = lax.axis_index("mem") * mem_dev
    tinv_mine = lax.dynamic_slice_in_dim(chol_inverse, first, mem_dev, 0).T
    mix_w = (weights[:, None] * scale + tinv_mine).astype(jnp.bfloat16)
    moved = jnp.einsum("kcm,mj->kcj", every_pertb, mix_w, preferred_element_type=jnp.float32)
    return (profile_average[:, :, None] + moved).astype(jnp.bfloat16)


def solution(mesh):
    placed = (
        P("cols", None, "mem"),
        P(),
        P(),
        P(),
        P(),
        P("cols", None),
        P("cols", None),
        P("cols", None),
        P("cols", None),
        P("cols"),
    )
    return jax.shard_map(
        body, mesh=mesh, in_specs=placed, out_specs=P("cols", None, "mem"), check_vma=False
    )
```
